128 devices in a mesh: seq: 32 (over x, y, core), sub: 4 (over z).
Axes of the slice: x: 4, y: 4, z: 4, core: 2. Of those that a mesh axis runs over, the one named last changes fastest.
Arguments:
- latents: bfloat16 [128, 1024, 320], P(('seq', 'sub')), may hold values from -16 to 16, as said below
- norm_gain: float32 [320], replicated, may hold values from 0.5 to 1.5
- norm_bias: float32 [320], replicated, may hold values from -3 to 3
- conv_weight: bfloat16 [3, 320, 320], replicated, may hold values from -0.1875 to 0.1875
- conv_bias: float32 [320], replicated, may hold values from -3 to 3
- query_weight: bfloat16 [320, 320], replicated, may hold values from -0.3125 to 0.3125
- key_weight: bfloat16 [320, 320], replicated, may hold values from -0.3125 to 0.3125
- value_weight: bfloat16 [320, 320], replicated, may hold values from -0.3125 to 0.3125
- out_weight: bfloat16 [320, 320], replicated, may hold values from -0.3125 to 0.3125
- pos_table: float32 [5, 63, 63], replicated, may hold values from -4 to 500
Outputs:
- block_out: bfloat16 [128, 1024, 320], P(('seq', 'sub'))
The draws below stay inside these ranges and needn't reach their ends.
Inputs may be any that keep to these rules, and one draw needn't show every extreme that they name: `latents`: a bounded latent field.
All inputs are finite; a program needn't handle non-finite values.
Results may differ from the reference program's by a relative error of at most 0.0066.
Values may be sent and summed in bfloat16 or wider, within the bound.
No kernel may reach another device: no remote copies, remote signals or barrier semaphores. Data moves between devices by JAX's collectives and lax.ppermute only.
A program may use at most 256 MiB of HBM per device.

```python
import jax
import jax.numpy as jnp
from jax import lax

SIDE = 32
C = 320
HEADS = 5
HEAD_DIM = 64
GROUPS = 32
FRAMES = 128


def draw_latents(key, part):
    ramp = jnp.arange(FRAMES, dtype=jnp.float32) / max(FRAMES - 1, 1)
    base = jnp.clip(jax.random.normal(key, (FRAMES, SIDE * SIDE, C), jnp.float32), -4.0, 4.0)
    factor = 3.0 - 2.0 * ramp
    return (base * factor[:, None, None]).astype(jnp.bfloat16)


def draw_pos_table(key, part):
    span = 2 * SIDE - 1
    table = jnp.clip(jax.random.normal(key, (HEADS, span, span), jnp.float32), -4.0, 4.0)
    return table


def centred(own_key, shape, deviation, bound, kind=jnp.bfloat16):
    entries = jax.random.normal(own_key, shape, jnp.float32) * deviation
    return jnp.minimum(jnp.maximum(entries, -bound), bound).astype(kind)


def setup_inputs(seed: int = 0) -> dict:
    seeds = jax.random.split(jax.random.key(seed), 11)
    return {
        "latents": draw_latents(jax.random.fold_in(seeds[10], 71), 0),
        "norm_gain": jnp.clip(1.0 + 0.1 * jax.random.normal(seeds[1], (C,), jnp.float32), 0.5, 1.5),
        "norm_bias": centred(seeds[2], (C,), 0.5, 3.0, jnp.float32),
        "conv_weight": centred(seeds[3], (3, C, C), (3 * C) ** -0.5, 0.1875),
        "conv_bias": centred(seeds[4], (C,), 0.5, 3.0, jnp.float32),
        "query_weight": centred(seeds[5], (C, C), C ** -0.5, 0.3125),
        "key_weight": centred(seeds[6], (C, C), C ** -0.5, 0.3125),
        "value_weight": centred(seeds[7], (C, C), C ** -0.5, 0.3125),
        "out_weight": centred(seeds[8], (C, C), C ** -0.5, 0.3125),
        "pos_table": draw_pos_table(jax.random.fold_in(seeds[10], 71), 0),
    }


EPS = 1e-05

def reference(latents, norm_gain, norm_bias, conv_weight, conv_bias, query_weight, key_weight, value_weight, out_weight, pos_table):
    frames, cells, width = latents.shape
    size = width // GROUPS
    grouped = latents.astype(jnp.float32).reshape(frames, cells, GROUPS, size)
    count = frames * cells * size
    mean = lax.optimization_barrier(jnp.sum(grouped, axis=(0, 1, 3))) / count
    meansq = lax.optimization_barrier(jnp.sum(grouped * grouped, axis=(0, 1, 3))) / count
    inv = lax.rsqrt(meansq - mean * mean + EPS)
    mean_c = jnp.repeat(mean, size)
    inv_c = jnp.repeat(inv, size)
    normed = ((latents.astype(jnp.float32) - mean_c) * inv_c * norm_gain + norm_bias).astype(jnp.bfloat16)
    padded = jnp.pad(normed, ((1, 1), (0, 0), (0, 0)))
    acc = jnp.zeros((frames * cells, width), jnp.float32)
    for tap in range(3):
        acc = acc + jnp.dot(padded[tap:tap + frames].reshape(-1, width), conv_weight[tap], preferred_element_type=jnp.float32)
    mixed = (normed.reshape(-1, width).astype(jnp.float32) + acc + conv_bias).astype(jnp.bfloat16)
    queries = jnp.dot(mixed, query_weight, preferred_element_type=jnp.float32).astype(jnp.bfloat16).reshape(frames, cells, width)
    keys = jnp.dot(mixed, key_weight, preferred_element_type=jnp.float32).astype(jnp.bfloat16).reshape(frames, cells, width)
    values = jnp.dot(mixed, value_weight, preferred_element_type=jnp.float32).astype(jnp.bfloat16).reshape(frames, cells, width)
    places = jnp.arange(cells, dtype=jnp.int32)
    row_pos = places // SIDE
    col_pos = places % SIDE
    delta_y = row_pos[:, None] - row_pos[None, :] + SIDE - 1
    delta_x = col_pos[:, None] - col_pos[None, :] + SIDE - 1
    bias_all = pos_table[:, delta_y, delta_x]
    scale = HEAD_DIM ** (-0.5)

    def attend_frame(index):
        prev_index = jnp.maximum(index - 1, 0)
        query_f = queries[index]
        key_f = jnp.concatenate([keys[0], keys[prev_index]], 0)
        value_f = jnp.concatenate([values[0], values[prev_index]], 0)
        outputs = []
        for head in range(HEADS):
            cols = slice(head * HEAD_DIM, (head + 1) * HEAD_DIM)
            scores = jnp.dot(query_f[:, cols], key_f[:, cols].T, preferred_element_type=jnp.float32) * scale
            scores = scores + jnp.concatenate([bias_all[head], bias_all[head]], 1)
            peak = lax.optimization_barrier(jnp.max(scores, axis=1, keepdims=True))
            weights = jnp.exp(scores - peak)
            probs = (weights / lax.optimization_barrier(jnp.sum(weights, axis=1, keepdims=True))).astype(jnp.bfloat16)
            outputs.append(jnp.dot(probs, value_f[:, cols], preferred_element_type=jnp.float32).astype(jnp.bfloat16))
        return jnp.concatenate(outputs, 1)
    attended = lax.map(attend_frame, jnp.arange(frames, dtype=jnp.int32))
    result = latents.reshape(-1, width).astype(jnp.float32) + jnp.dot(attended.reshape(-1, width), out_weight, preferred_element_type=jnp.float32)
    return result.astype(jnp.bfloat16).reshape(frames, cells, width)
```

```python
import numpy as np
import jax
import jax.numpy as jnp
from jax import lax
from jax.sharding import PartitionSpec as P

SIDE = 32
HEAD_DIM = 64
GROUPS = 32

EPS = 1e-05
AXES = ("seq", "sub")


def place_of():
    return lax.axis_index("seq") * lax.axis_size("sub") + lax.axis_index("sub")


def shifted(array, devices, by):
    pairs = [(i, i + by) for i in range(devices) if 0 <= i + by < devices]
    return lax.ppermute(array, AXES, pairs)


def butterfly_sum(x, devices):
    step = 1
    while step < devices:
        x = x + lax.ppermute(x, AXES, [(i, i ^ step) for i in range(devices)])
        step *= 2
    return x


def broadcast_pair(first, second, place, devices):
    step = 2
    while step < devices:
        got_a = lax.ppermute(first, AXES, [(i, i + step) for i in range(0, step, 2)])
        got_b = lax.ppermute(second, AXES, [(i, i + step) for i in range(1, step, 2)])
        fresh = (place >= step) & (place < 2 * step)
        first = jnp.where(fresh & (place % 2 == 0), got_a, first)
        second = jnp.where(fresh & (place % 2 == 1), got_b, second)
        step *= 2
    swap_a = lax.ppermute(first, AXES, [(i, i ^ 1) for i in range(devices)])
    swap_b = lax.ppermute(second, AXES, [(i, i ^ 1) for i in range(devices)])
    even = place % 2 == 0
    return jnp.where(even, first, swap_a), jnp.where(even, swap_b, second)


def position_bias(pos_table):
    coord = np.arange(SIDE)
    ix = coord[:, None] - coord[None, :] + SIDE - 1
    t1 = pos_table[:, :, ix]
    u = jnp.transpose(t1[:, ::-1], (0, 2, 1, 3))
    rows = [
        u[:, :, SIDE - 1 - py : 2 * SIDE - 1 - py, :].reshape(u.shape[0], SIDE, SIDE * SIDE)
        for py in range(SIDE)
    ]
    return jnp.stack(rows, 1).reshape(u.shape[0], SIDE * SIDE, SIDE * SIDE)


def project(rows, weight):
    return jnp.dot(rows, weight, preferred_element_type=jnp.float32).astype(jnp.bfloat16)


def body(
    latents,
    norm_gain,
    norm_bias,
    conv_weight,
    conv_bias,
    query_weight,
    key_weight,
    value_weight,
    out_weight,
    pos_table,
):
    frames, cells, width = latents.shape
    size = width // GROUPS
    devices = lax.axis_size("seq") * lax.axis_size("sub")
    place = place_of()
    own = latents[0]

    before = shifted(own, devices, 1)
    before2 = shifted(own, devices, 2)
    after = shifted(own, devices, -1)
    frame0, frame1 = broadcast_pair(own, own, place, devices)

    grouped = own.reshape(cells, GROUPS, size).astype(jnp.float32)
    partial = jnp.concatenate([jnp.sum(grouped, axis=(0, 2)), jnp.sum(grouped * grouped, axis=(0, 2))])
    stats = butterfly_sum(partial, devices)
    count = frames * devices * cells * size
    mean = stats[:GROUPS] / count
    meansq = stats[GROUPS:] / count
    inv = lax.rsqrt(meansq - mean * mean + EPS)
    mean_c = jnp.repeat(mean, size)
    inv_c = jnp.repeat(inv, size)

    def norm(x):
        return ((x.astype(jnp.float32) - mean_c) * inv_c * norm_gain + norm_bias).astype(jnp.bfloat16)

    zero = jnp.zeros((cells, width), jnp.bfloat16)
    n_self = norm(own)
    n_before = jnp.where(place >= 1, norm(before), zero)
    n_before2 = jnp.where(place >= 2, norm(before2), zero)
    n_after = jnp.where(place + 1 < devices, norm(after), zero)
    n_0 = norm(frame0)
    n_1 = norm(frame1)

    taps = [
        jnp.concatenate([n_before2, n_before, zero], 0),
        jnp.concatenate([n_before, n_self, n_0], 0),
        jnp.concatenate([n_self, n_after, n_1], 0),
    ]
    acc = jnp.zeros((3 * cells, width), jnp.float32)
    for tap in range(3):
        acc = acc + jnp.dot(taps[tap], conv_weight[tap], preferred_element_type=jnp.float32)
    mixed = (taps[1].astype(jnp.float32) + acc + conv_bias).astype(jnp.bfloat16)
    mixed_prev = mixed[:cells]
    mixed_self = mixed[cells : 2 * cells]
    mixed_first = mixed[2 * cells :]

    queries = project(mixed_self, query_weight)
    kv_rows = jnp.concatenate([mixed_prev, mixed_first], 0)
    keys2 = project(kv_rows, key_weight)
    values2 = project(kv_rows, value_weight)
    leading = place <= 1
    prev_key = jnp.where(leading, keys2[cells:], keys2[:cells])
    prev_value = jnp.where(leading, values2[cells:], values2[:cells])
    first_key = keys2[cells:]
    first_value = values2[cells:]

    bias_all = position_bias(pos_table)
    scale = HEAD_DIM ** (-0.5)
    per_head = []
    for head in range(width // HEAD_DIM):
        cols = slice(head * HEAD_DIM, (head + 1) * HEAD_DIM)
        bias_head = bias_all[head]
        key_block = jnp.concatenate([first_key[:, cols], prev_key[:, cols]], 0)
        value_block = jnp.concatenate([first_value[:, cols], prev_value[:, cols]], 0)
        scores = jnp.dot(queries[:, cols], key_block.T, preferred_element_type=jnp.float32) * scale
        scores = (scores.reshape(cells, 2, cells) + bias_head[:, None, :]).reshape(cells, 2 * cells)
        peak = jnp.max(scores, axis=1, keepdims=True)
        weights = jnp.exp(scores - peak)
        probs = (weights / jnp.sum(weights, axis=1, keepdims=True)).astype(jnp.bfloat16)
        per_head.append(jnp.dot(probs, value_block, preferred_element_type=jnp.float32).astype(jnp.bfloat16))
    attended = jnp.concatenate(per_head, 1)
    result = own.astype(jnp.float32) + jnp.dot(attended, out_weight, preferred_element_type=jnp.float32)
    return result.astype(jnp.bfloat16).reshape(frames, cells, width)


def solution(mesh):
    return jax.shard_map(
        body,
        mesh=mesh,
        in_specs=(P(AXES, None, None), P(), P(), P(), P(), P(), P(), P(), P(), P()),
        out_specs=P(AXES, None, None),
        check_vma=False,
    )
```

```python
import numpy as np
import jax
import jax.numpy as jnp
from jax import lax
from jax.sharding import PartitionSpec as P

SIDE = 32
HEAD_DIM = 64
GROUPS = 32

EPS = 1e-05
AXES = ("seq", "sub")


def place_of():
    return lax.axis_index("seq") * lax.axis_size("sub") + lax.axis_index("sub")


def shifted(array, devices, by):
    pairs = [(i, i + by) for i in range(devices) if 0 <= i + by < devices]
    return lax.ppermute(array, AXES, pairs)


def butterfly_sum(x, devices):
    step = 1
    while step < devices:
        x = x + lax.ppermute(x, AXES, [(i, i ^ step) for i in range(devices)])
        step *= 2
    return x


def broadcast_pair(first, second, place, devices):
    step = 2
    while step < devices:
        got_a = lax.ppermute(first, AXES, [(i, i + step) for i in range(0, step, 2)])
        got_b = lax.ppermute(second, AXES, [(i, i + step) for i in range(1, step, 2)])
        fresh = (place >= step) & (place < 2 * step)
        first = jnp.where(fresh & (place % 2 == 0), got_a, first)
        second = jnp.where(fresh & (place % 2 == 1), got_b, second)
        step *= 2
    swap_a = lax.ppermute(first, AXES, [(i, i ^ 1) for i in range(devices)])
    swap_b = lax.ppermute(second, AXES, [(i, i ^ 1) for i in range(devices)])
    even = place % 2 == 0
    return jnp.where(even, first, swap_a), jnp.where(even, swap_b, second)


def position_bias(pos_table):
    heads, span, _ = pos_table.shape
    coord = np.arange(SIDE)
    k = np.arange(span)
    dy = (span - 1 - k)[None, :, None]
    dx = (coord[:, None, None] - coord[None, None, :] + SIDE - 1)
    flat_index = (dy * span + dx).reshape(SIDE, span * SIDE)
    wide = pos_table.reshape(heads, span * span)[:, flat_index]
    lanes = 128
    per = lanes // SIDE
    width = (SIDE - 1) // per * lanes + SIDE * SIDE
    shifted = [wide[:, :, SIDE * s : SIDE * s + width] for s in range(per)]
    rows = []
    for py in range(SIDE):
        start = (SIDE - 1 - py) * SIDE
        piece = shifted[start % lanes // SIDE]
        base = start // lanes * lanes
        rows.append(piece[:, :, base : base + SIDE * SIDE])
    return jnp.concatenate(rows, 1)


def project(rows, weight):
    return jnp.dot(rows, weight, preferred_element_type=jnp.float32).astype(jnp.bfloat16)


def body(
    latents,
    norm_gain,
    norm_bias,
    conv_weight,
    conv_bias,
    query_weight,
    key_weight,
    value_weight,
    out_weight,
    pos_table,
):
    frames, cells, width = latents.shape
    size = width // GROUPS
    devices = lax.axis_size("seq") * lax.axis_size("sub")
    place = place_of()
    own = latents[0]

    before = shifted(own, devices, 1)
    before2 = shifted(own, devices, 2)
    after = shifted(own, devices, -1)
    frame0, frame1 = broadcast_pair(own, own, place, devices)

    grouped = own.reshape(cells, GROUPS, size).astype(jnp.float32)
    partial = jnp.concatenate([jnp.sum(grouped, axis=(0, 2)), jnp.sum(grouped * grouped, axis=(0, 2))])
    stats = butterfly_sum(partial, devices)
    count = frames * devices * cells * size
    mean = stats[:GROUPS] / count
    meansq = stats[GROUPS:] / count
    inv = lax.rsqrt(meansq - mean * mean + EPS)
    mean_c = jnp.repeat(mean, size)
    inv_c = jnp.repeat(inv, size)

    def norm(x):
        return ((x.astype(jnp.float32) - mean_c) * inv_c * norm_gain + norm_bias).astype(jnp.bfloat16)

    zero = jnp.zeros((cells, width), jnp.bfloat16)
    n_self = norm(own)
    n_before = jnp.where(place >= 1, norm(before), zero)
    n_before2 = jnp.where(place >= 2, norm(before2), zero)
    n_after = jnp.where(place + 1 < devices, norm(after), zero)
    n_0 = norm(frame0)
    n_1 = norm(frame1)

    taps = [
        jnp.concatenate([n_before2, n_before, zero], 0),
        jnp.concatenate([n_before, n_self, n_0], 0),
        jnp.concatenate([n_self, n_after, n_1], 0),
    ]
    acc = jnp.zeros((3 * cells, width), jnp.float32)
    for tap in range(3):
        acc = acc + jnp.dot(taps[tap], conv_weight[tap], preferred_element_type=jnp.float32)
    mixed = (taps[1].astype(jnp.float32) + acc + conv_bias).astype(jnp.bfloat16)
    mixed_prev = mixed[:cells]
    mixed_self = mixed[cells : 2 * cells]
    mixed_first = mixed[2 * cells :]

    queries = project(mixed_self, query_weight)
    kv_rows = jnp.concatenate([mixed_prev, mixed_first], 0)
    keys2 = project(kv_rows, key_weight)
    values2 = project(kv_rows, value_weight)
    leading = place <= 1
    prev_key = jnp.where(leading, keys2[cells:], keys2[:cells])
    prev_value = jnp.where(leading, values2[cells:], values2[:cells])
    first_key = keys2[cells:]
    first_value = values2[cells:]

    bias_all = position_bias(pos_table)
    scale = HEAD_DIM ** (-0.5)
    per_head = []
    for head in range(width // HEAD_DIM):
        cols = slice(head * HEAD_DIM, (head + 1) * HEAD_DIM)
        bias_head = bias_all[head]
        key_block = jnp.concatenate([first_key[:, cols], prev_key[:, cols]], 0)
        value_block = jnp.concatenate([first_value[:, cols], prev_value[:, cols]], 0)
        scores = jnp.dot(queries[:, cols], key_block.T, preferred_element_type=jnp.float32) * scale
        scores = (scores.reshape(cells, 2, cells) + bias_head[:, None, :]).reshape(cells, 2 * cells)
        peak = jnp.max(scores, axis=1, keepdims=True)
        weights = jnp.exp(scores - peak)
        probs = (weights / jnp.sum(weights, axis=1, keepdims=True)).astype(jnp.bfloat16)
        per_head.append(jnp.dot(probs, value_block, preferred_element_type=jnp.float32).astype(jnp.bfloat16))
    attended = jnp.concatenate(per_head, 1)
    result = own.astype(jnp.float32) + jnp.dot(attended, out_weight, preferred_element_type=jnp.float32)
    return result.astype(jnp.bfloat16).reshape(frames, cells, width)


def solution(mesh):
    return jax.shard_map(
        body,
        mesh=mesh,
        in_specs=(P(AXES, None, None), P(), P(), P(), P(), P(), P(), P(), P(), P()),
        out_specs=P(AXES, None, None),
        check_vma=False,
    )
```

```python
import numpy as np
import jax
import jax.numpy as jnp
from jax import lax
from jax.sharding import PartitionSpec as P

SIDE = 32
HEAD_DIM = 64
GROUPS = 32

EPS = 1e-05
AXES = ("seq", "sub")


def place_of():
    return lax.axis_index("seq") * lax.axis_size("sub") + lax.axis_index("sub")


def shifted(array, devices, by):
    pairs = [(i, i + by) for i in range(devices) if 0 <= i + by < devices]
    return lax.ppermute(array, AXES, pairs)


def butterfly_sum(x, devices):
    step = 1
    while step < devices:
        x = x + lax.ppermute(x, AXES, [(i, i ^ step) for i in range(devices)])
        step *= 2
    return x


def broadcast_pair(first, second, place, devices):
    step = 2
    while step < devices:
        got_a = lax.ppermute(first, AXES, [(i, i + step) for i in range(0, step, 2)])
        got_b = lax.ppermute(second, AXES, [(i, i + step) for i in range(1, step, 2)])
        fresh = (place >= step) & (place < 2 * step)
        first = jnp.where(fresh & (place % 2 == 0), got_a, first)
        second = jnp.where(fresh & (place % 2 == 1), got_b, second)
        step *= 2
    swap_a = lax.ppermute(first, AXES, [(i, i ^ 1) for i in range(devices)])
    swap_b = lax.ppermute(second, AXES, [(i, i ^ 1) for i in range(devices)])
    even = place % 2 == 0
    return jnp.where(even, first, swap_a), jnp.where(even, swap_b, second)


def position_bias(pos_table):
    heads, span, _ = pos_table.shape
    flipped = pos_table[:, ::-1, ::-1]
    windows = [flipped[:, :, SIDE - 1 - px : span - px] for px in range(SIDE)]
    wide = jnp.stack(windows, 1).reshape(heads, SIDE, span * SIDE)
    lanes = 128
    per = lanes // SIDE
    width = (SIDE - 1) // per * lanes + SIDE * SIDE
    shifted = [wide[:, :, SIDE * s : SIDE * s + width] for s in range(per)]
    rows = []
    for py in range(SIDE):
        start = (SIDE - 1 - py) * SIDE
        piece = shifted[start % lanes // SIDE]
        base = start // lanes * lanes
        rows.append(piece[:, :, base : base + SIDE * SIDE])
    return jnp.concatenate(rows, 1)


def project(rows, weight):
    return jnp.dot(rows, weight, preferred_element_type=jnp.float32).astype(jnp.bfloat16)


def body(
    latents,
    norm_gain,
    norm_bias,
    conv_weight,
    conv_bias,
    query_weight,
    key_weight,
    value_weight,
    out_weight,
    pos_table,
):
    frames, cells, width = latents.shape
    size = width // GROUPS
    devices = lax.axis_size("seq") * lax.axis_size("sub")
    place = place_of()
    own = latents[0]

    before = shifted(own, devices, 1)
    before2 = shifted(own, devices, 2)
    after = shifted(own, devices, -1)
    frame0, frame1 = broadcast_pair(own, own, place, devices)

    grouped = own.reshape(cells, GROUPS, size).astype(jnp.float32)
    partial = jnp.concatenate([jnp.sum(grouped, axis=(0, 2)), jnp.sum(grouped * grouped, axis=(0, 2))])
    stats = butterfly_sum(partial, devices)
    count = frames * devices * cells * size
    mean = stats[:GROUPS] / count
    meansq = stats[GROUPS:] / count
    inv = lax.rsqrt(meansq - mean * mean + EPS)
    mean_c = jnp.repeat(mean, size)
    inv_c = jnp.repeat(inv, size)

    def norm(x):
        return ((x.astype(jnp.float32) - mean_c) * inv_c * norm_gain + norm_bias).astype(jnp.bfloat16)

    zero = jnp.zeros((cells, width), jnp.bfloat16)
    n_self = norm(own)
    n_before = jnp.where(place >= 1, norm(before), zero)
    n_before2 = jnp.where(place >= 2, norm(before2), zero)
    n_after = jnp.where(place + 1 < devices, norm(after), zero)
    n_0 = norm(frame0)
    n_1 = norm(frame1)

    taps = [
        jnp.concatenate([n_before2, n_before, zero], 0),
        jnp.concatenate([n_before, n_self, n_0], 0),
        jnp.concatenate([n_self, n_after, n_1], 0),
    ]
    acc = jnp.zeros((3 * cells, width), jnp.float32)
    for tap in range(3):
        acc = acc + jnp.dot(taps[tap], conv_weight[tap], preferred_element_type=jnp.float32)
    mixed = (taps[1].astype(jnp.float32) + acc + conv_bias).astype(jnp.bfloat16)
    mixed_prev = mixed[:cells]
    mixed_self = mixed[cells : 2 * cells]
    mixed_first = mixed[2 * cells :]

    queries = project(mixed_self, query_weight)
    kv_rows = jnp.concatenate([mixed_prev, mixed_first], 0)
    keys2 = project(kv_rows, key_weight)
    values2 = project(kv_rows, value_weight)
    leading = place <= 1
    prev_key = jnp.where(leading, keys2[cells:], keys2[:cells])
    prev_value = jnp.where(leading, values2[cells:], values2[:cells])
    first_key = keys2[cells:]
    first_value = values2[cells:]

    bias_all = position_bias(pos_table)
    scale = HEAD_DIM ** (-0.5)
    per_head = []
    for head in range(width // HEAD_DIM):
        cols = slice(head * HEAD_DIM, (head + 1) * HEAD_DIM)
        bias_head = bias_all[head]
        key_block = jnp.concatenate([first_key[:, cols], prev_key[:, cols]], 0)
        value_block = jnp.concatenate([first_value[:, cols], prev_value[:, cols]], 0)
        scores = jnp.dot(queries[:, cols], key_block.T, preferred_element_type=jnp.float32) * scale
        scores = (scores.reshape(cells, 2, cells) + bias_head[:, None, :]).reshape(cells, 2 * cells)
        peak = jnp.max(scores, axis=1, keepdims=True)
        weights = jnp.exp(scores - peak)
        probs = (weights / jnp.sum(weights, axis=1, keepdims=True)).astype(jnp.bfloat16)
        per_head.append(jnp.dot(probs, value_block, preferred_element_type=jnp.float32).astype(jnp.bfloat16))
    attended = jnp.concatenate(per_head, 1)
    result = own.astype(jnp.float32) + jnp.dot(attended, out_weight, preferred_element_type=jnp.float32)
    return result.astype(jnp.bfloat16).reshape(frames, cells, width)


def solution(mesh):
    return jax.shard_map(
        body,
        mesh=mesh,
        in_specs=(P(AXES, None, None), P(), P(), P(), P(), P(), P(), P(), P(), P()),
        out_specs=P(AXES, None, None),
        check_vma=False,
    )
```

```python
import numpy as np
import jax
import jax.numpy as jnp
from jax import lax
from jax.sharding import PartitionSpec as P

SIDE = 32
HEAD_DIM = 64
GROUPS = 32

EPS = 1e-05
AXES = ("seq", "sub")


def place_of():
    return lax.axis_index("seq") * lax.axis_size("sub") + lax.axis_index("sub")


def shifted(array, devices, by):
    pairs = [(i, i + by) for i in range(devices) if 0 <= i + by < devices]
    return lax.ppermute(array, AXES, pairs)


def butterfly_sum(x, devices):
    step = 1
    while step < devices:
        x = x + lax.ppermute(x, AXES, [(i, i ^ step) for i in range(devices)])
        step *= 2
    return x


def broadcast_pair(first, second, place, devices):
    step = 2
    while step < devices:
        got_a = lax.ppermute(first, AXES, [(i, i + step) for i in range(0, step, 2)])
        got_b = lax.ppermute(second, AXES, [(i, i + step) for i in range(1, step, 2)])
        fresh = (place >= step) & (place < 2 * step)
        first = jnp.where(fresh & (place % 2 == 0), got_a, first)
        second = jnp.where(fresh & (place % 2 == 1), got_b, second)
        step *= 2
    swap_a = lax.ppermute(first, AXES, [(i, i ^ 1) for i in range(devices)])
    swap_b = lax.ppermute(second, AXES, [(i, i ^ 1) for i in range(devices)])
    even = place % 2 == 0
    return jnp.where(even, first, swap_a), jnp.where(even, swap_b, second)


def position_bias(pos_table):
    heads, span, _ = pos_table.shape
    flipped = pos_table[:, ::-1, ::-1]
    coord = np.arange(SIDE)
    pick = np.arange(span)[:, None, None] == (SIDE - 1 - coord[:, None] + coord[None, :])[None]
    pick = jnp.asarray(pick.reshape(span, SIDE * SIDE), jnp.float32)
    table = jnp.einsum("hkj,jc->hkc", flipped, pick, precision=lax.Precision.HIGHEST)
    wide = jnp.transpose(table.reshape(heads, span, SIDE, SIDE), (0, 2, 1, 3))
    wide = wide.reshape(heads, SIDE, span * SIDE)
    lanes = 128
    per = lanes // SIDE
    width = (SIDE - 1) // per * lanes + SIDE * SIDE
    out = []
    for head in range(heads):
        shifted = [wide[head, :, SIDE * s : SIDE * s + width] for s in range(per)]
        rows = []
        for py in range(SIDE):
            start = (SIDE - 1 - py) * SIDE
            piece = shifted[start % lanes // SIDE]
            base = start // lanes * lanes
            rows.append(piece[:, base : base + SIDE * SIDE])
        out.append(jnp.concatenate(rows, 0))
    return out


def project(rows, weight):
    return jnp.dot(rows, weight, preferred_element_type=jnp.float32).astype(jnp.bfloat16)


def body(
    latents,
    norm_gain,
    norm_bias,
    conv_weight,
    conv_bias,
    query_weight,
    key_weight,
    value_weight,
    out_weight,
    pos_table,
):
    frames, cells, width = latents.shape
    size = width // GROUPS
    devices = lax.axis_size("seq") * lax.axis_size("sub")
    place = place_of()
    own = latents[0]

    before = shifted(own, devices, 1)
    before2 = shifted(own, devices, 2)
    after = shifted(own, devices, -1)
    frame0, frame1 = broadcast_pair(own, own, place, devices)

    grouped = own.reshape(cells, GROUPS, size).astype(jnp.float32)
    partial = jnp.concatenate([jnp.sum(grouped, axis=(0, 2)), jnp.sum(grouped * grouped, axis=(0, 2))])
    stats = butterfly_sum(partial, devices)
    count = frames * devices * cells * size
    mean = stats[:GROUPS] / count
    meansq = stats[GROUPS:] / count
    inv = lax.rsqrt(meansq - mean * mean + EPS)
    mean_c = jnp.repeat(mean, size)
    inv_c = jnp.repeat(inv, size)

    def norm(x):
        return ((x.astype(jnp.float32) - mean_c) * inv_c * norm_gain + norm_bias).astype(jnp.bfloat16)

    zero = jnp.zeros((cells, width), jnp.bfloat16)
    n_self = norm(own)
    n_before = jnp.where(place >= 1, norm(before), zero)
    n_before2 = jnp.where(place >= 2, norm(before2), zero)
    n_after = jnp.where(place + 1 < devices, norm(after), zero)
    n_0 = norm(frame0)
    n_1 = norm(frame1)

    taps = [
        jnp.concatenate([n_before2, n_before, zero], 0),
        jnp.concatenate([n_before, n_self, n_0], 0),
        jnp.concatenate([n_self, n_after, n_1], 0),
    ]
    acc = jnp.zeros((3 * cells, width), jnp.float32)
    for tap in range(3):
        acc = acc + jnp.dot(taps[tap], conv_weight[tap], preferred_element_type=jnp.float32)
    mixed = (taps[1].astype(jnp.float32) + acc + conv_bias).astype(jnp.bfloat16)
    mixed_prev = mixed[:cells]
    mixed_self = mixed[cells : 2 * cells]
    mixed_first = mixed[2 * cells :]

    queries = project(mixed_self, query_weight)
    kv_rows = jnp.concatenate([mixed_prev, mixed_first], 0)
    keys2 = project(kv_rows, key_weight)
    values2 = project(kv_rows, value_weight)
    leading = place <= 1
    prev_key = jnp.where(leading, keys2[cells:], keys2[:cells])
    prev_value = jnp.where(leading, values2[cells:], values2[:cells])
    first_key = keys2[cells:]
    first_value = values2[cells:]

    stats, pos_table = lax.optimization_barrier((stats, pos_table))
    bias_all = position_bias(pos_table)
    scale = HEAD_DIM ** (-0.5)
    per_head = []
    for head in range(width // HEAD_DIM):
        cols = slice(head * HEAD_DIM, (head + 1) * HEAD_DIM)
        bias_head = bias_all[head]
        key_block = jnp.concatenate([first_key[:, cols], prev_key[:, cols]], 0)
        value_block = jnp.concatenate([first_value[:, cols], prev_value[:, cols]], 0)
        scores = jnp.dot(queries[:, cols], key_block.T, preferred_element_type=jnp.float32) * scale
        scores = (scores.reshape(cells, 2, cells) + bias_head[:, None, :]).reshape(cells, 2 * cells)
        peak = jnp.max(scores, axis=1, keepdims=True)
        weights = jnp.exp(scores - peak)
        probs = (weights / jnp.sum(weights, axis=1, keepdims=True)).astype(jnp.bfloat16)
        per_head.append(jnp.dot(probs, value_block, preferred_element_type=jnp.float32).astype(jnp.bfloat16))
    attended = jnp.concatenate(per_head, 1)
    result = own.astype(jnp.float32) + jnp.dot(attended, out_weight, preferred_element_type=jnp.float32)
    return result.astype(jnp.bfloat16).reshape(frames, cells, width)


def solution(mesh):
    return jax.shard_map(
        body,
        mesh=mesh,
        in_specs=(P(AXES, None, None), P(), P(), P(), P(), P(), P(), P(), P(), P()),
        out_specs=P(AXES, None, None),
        check_vma=False,
    )
```

```python
import numpy as np
import jax
import jax.numpy as jnp
from jax import lax
from jax.sharding import PartitionSpec as P

SIDE = 32
HEAD_DIM = 64
GROUPS = 32

EPS = 1e-05
AXES = ("seq", "sub")


def place_of():
    return lax.axis_index("seq") * lax.axis_size("sub") + lax.axis_index("sub")


def shifted(array, devices, by):
    pairs = [(i, i + by) for i in range(devices) if 0 <= i + by < devices]
    return lax.ppermute(array, AXES, pairs)


def butterfly_sum(x, devices):
    step = 1
    while step < devices:
        x = x + lax.ppermute(x, AXES, [(i, i ^ step) for i in range(devices)])
        step *= 2
    return x


def broadcast_pair(first, second, place, devices, work):
    step = 2
    done = []
    while step < devices:
        got_a = lax.ppermute(first, AXES, [(i, i + step) for i in range(0, step, 2)])
        got_b = lax.ppermute(second, AXES, [(i, i + step) for i in range(1, step, 2)])
        fresh = (place >= step) & (place < 2 * step)
        first = jnp.where(fresh & (place % 2 == 0), got_a, first)
        second = jnp.where(fresh & (place % 2 == 1), got_b, second)
        if len(done) < len(work):
            first, second, operand = lax.optimization_barrier((first, second, work[len(done)][0]))
            done.append(work[len(done)][1](operand))
        step *= 2
    swap_a = lax.ppermute(first, AXES, [(i, i ^ 1) for i in range(devices)])
    swap_b = lax.ppermute(second, AXES, [(i, i ^ 1) for i in range(devices)])
    even = place % 2 == 0
    return jnp.where(even, first, swap_a), jnp.where(even, swap_b, second), done


def bias_table(pos_table):
    heads, span, _ = pos_table.shape
    flipped = pos_table[:, ::-1, ::-1]
    coord = np.arange(SIDE)
    pick = np.arange(span)[:, None, None] == (SIDE - 1 - coord[:, None] + coord[None, :])[None]
    pick = jnp.asarray(pick.reshape(span, SIDE * SIDE), jnp.float32)
    table = jnp.einsum("hkj,jc->hkc", flipped, pick, precision=lax.Precision.HIGHEST)
    wide = jnp.transpose(table.reshape(heads, span, SIDE, SIDE), (0, 2, 1, 3))
    wide = wide.reshape(heads, SIDE, span * SIDE)
    return wide


def head_bias(wide_head):
    lanes = 128
    per = lanes // SIDE
    width = (SIDE - 1) // per * lanes + SIDE * SIDE
    shifted = [wide_head[:, SIDE * s : SIDE * s + width] for s in range(per)]
    rows = []
    for py in range(SIDE):
        start = (SIDE - 1 - py) * SIDE
        piece = shifted[start % lanes // SIDE]
        base = start // lanes * lanes
        rows.append(piece[:, base : base + SIDE * SIDE])
    return jnp.concatenate(rows, 0)


def project(rows, weight):
    return jnp.dot(rows, weight, preferred_element_type=jnp.float32).astype(jnp.bfloat16)


def body(
    latents,
    norm_gain,
    norm_bias,
    conv_weight,
    conv_bias,
    query_weight,
    key_weight,
    value_weight,
    out_weight,
    pos_table,
):
    frames, cells, width = latents.shape
    size = width // GROUPS
    devices = lax.axis_size("seq") * lax.axis_size("sub")
    place = place_of()
    own = latents[0]

    before = shifted(own, devices, 1)
    before2 = shifted(own, devices, 2)
    after = shifted(own, devices, -1)

    grouped = own.reshape(cells, GROUPS, size).astype(jnp.float32)
    partial = jnp.concatenate([jnp.sum(grouped, axis=(0, 2)), jnp.sum(grouped * grouped, axis=(0, 2))])
    stats = butterfly_sum(partial, devices)
    count = frames * devices * cells * size
    stats, pos_table = lax.optimization_barrier((stats, pos_table))
    wide = bias_table(pos_table)
    work = [(wide[h], head_bias) for h in range(wide.shape[0])]
    frame0, frame1, bias_all = broadcast_pair(own, own, place, devices, work)
    mean = stats[:GROUPS] / count
    meansq = stats[GROUPS:] / count
    inv = lax.rsqrt(meansq - mean * mean + EPS)
    mean_c = jnp.repeat(mean, size)
    inv_c = jnp.repeat(inv, size)

    def norm(x):
        return ((x.astype(jnp.float32) - mean_c) * inv_c * norm_gain + norm_bias).astype(jnp.bfloat16)

    zero = jnp.zeros((cells, width), jnp.bfloat16)
    n_self = norm(own)
    n_before = jnp.where(place >= 1, norm(before), zero)
    n_before2 = jnp.where(place >= 2, norm(before2), zero)
    n_after = jnp.where(place + 1 < devices, norm(after), zero)
    n_0 = norm(frame0)
    n_1 = norm(frame1)

    taps = [
        jnp.concatenate([n_before2, n_before, zero], 0),
        jnp.concatenate([n_before, n_self, n_0], 0),
        jnp.concatenate([n_self, n_after, n_1], 0),
    ]
    acc = jnp.zeros((3 * cells, width), jnp.float32)
    for tap in range(3):
        acc = acc + jnp.dot(taps[tap], conv_weight[tap], preferred_element_type=jnp.float32)
    mixed = (taps[1].astype(jnp.float32) + acc + conv_bias).astype(jnp.bfloat16)
    mixed_prev = mixed[:cells]
    mixed_self = mixed[cells : 2 * cells]
    mixed_first = mixed[2 * cells :]

    queries = project(mixed_self, query_weight)
    kv_rows = jnp.concatenate([mixed_prev, mixed_first], 0)
    keys2 = project(kv_rows, key_weight)
    values2 = project(kv_rows, value_weight)
    leading = place <= 1
    prev_key = jnp.where(leading, keys2[cells:], keys2[:cells])
    prev_value = jnp.where(leading, values2[cells:], values2[:cells])
    first_key = keys2[cells:]
    first_value = values2[cells:]

    scale = HEAD_DIM ** (-0.5)
    per_head = []
    for head in range(width // HEAD_DIM):
        cols = slice(head * HEAD_DIM, (head + 1) * HEAD_DIM)
        bias_head = bias_all[head]
        key_block = jnp.concatenate([first_key[:, cols], prev_key[:, cols]], 0)
        value_block = jnp.concatenate([first_value[:, cols], prev_value[:, cols]], 0)
        scores = jnp.dot(queries[:, cols], key_block.T, preferred_element_type=jnp.float32) * scale
        scores = (scores.reshape(cells, 2, cells) + bias_head[:, None, :]).reshape(cells, 2 * cells)
        peak = jnp.max(scores, axis=1, keepdims=True)
        weights = jnp.exp(scores - peak)
        probs = (weights / jnp.sum(weights, axis=1, keepdims=True)).astype(jnp.bfloat16)
        per_head.append(jnp.dot(probs, value_block, preferred_element_type=jnp.float32).astype(jnp.bfloat16))
    attended = jnp.concatenate(per_head, 1)
    result = own.astype(jnp.float32) + jnp.dot(attended, out_weight, preferred_element_type=jnp.float32)
    return result.astype(jnp.bfloat16).reshape(frames, cells, width)


def solution(mesh):
    return jax.shard_map(
        body,
        mesh=mesh,
        in_specs=(P(AXES, None, None), P(), P(), P(), P(), P(), P(), P(), P(), P()),
        out_specs=P(AXES, None, None),
        check_vma=False,
    )
```

```python
import numpy as np
import jax
import jax.numpy as jnp
from jax import lax
from jax.sharding import PartitionSpec as P

SIDE = 32
HEAD_DIM = 64
GROUPS = 32

EPS = 1e-05
AXES = ("seq", "sub")


def place_of():
    return lax.axis_index("seq") * lax.axis_size("sub") + lax.axis_index("sub")


def shifted(array, devices, by):
    pairs = [(i, i + by) for i in range(devices) if 0 <= i + by < devices]
    return lax.ppermute(array, AXES, pairs)


def butterfly_sum(x, devices):
    step = 1
    while step < devices:
        x = x + lax.ppermute(x, AXES, [(i, i ^ step) for i in range(devices)])
        step *= 2
    return x


def broadcast_pair(first, second, place, devices, work):
    step = 2
    done = []
    while step < devices:
        got_a = lax.ppermute(first, AXES, [(i, i + step) for i in range(0, step, 2)])
        got_b = lax.ppermute(second, AXES, [(i, i + step) for i in range(1, step, 2)])
        fresh = (place >= step) & (place < 2 * step)
        first = jnp.where(fresh & (place % 2 == 0), got_a, first)
        second = jnp.where(fresh & (place % 2 == 1), got_b, second)
        if len(done) < len(work):
            first, second, operand = lax.optimization_barrier((first, second, work[len(done)][0]))
            done.append(work[len(done)][1](operand))
        step *= 2
    swap_a = lax.ppermute(first, AXES, [(i, i ^ 1) for i in range(devices)])
    swap_b = lax.ppermute(second, AXES, [(i, i ^ 1) for i in range(devices)])
    even = place % 2 == 0
    return jnp.where(even, first, swap_a), jnp.where(even, swap_b, second), done


def bias_table(pos_table):
    heads, span, _ = pos_table.shape
    flipped = pos_table[:, ::-1, ::-1]
    coord = np.arange(SIDE)
    pick = np.arange(span)[:, None, None] == (SIDE - 1 - coord[:, None] + coord[None, :])[None]
    pick = jnp.asarray(pick.reshape(span, SIDE * SIDE), jnp.float32)
    table = jnp.einsum("hkj,jc->hkc", flipped, pick, precision=lax.Precision.HIGHEST)
    wide = jnp.transpose(table.reshape(heads, span, SIDE, SIDE), (0, 2, 1, 3))
    wide = wide.reshape(heads, SIDE, span * SIDE)
    return wide


def head_bias(wide_head):
    lanes = 128
    per = lanes // SIDE
    width = (SIDE - 1) // per * lanes + SIDE * SIDE
    shifted = [wide_head[:, SIDE * s : SIDE * s + width] for s in range(per)]
    rows = []
    for py in range(SIDE):
        start = (SIDE - 1 - py) * SIDE
        piece = shifted[start % lanes // SIDE]
        base = start // lanes * lanes
        rows.append(piece[:, base : base + SIDE * SIDE])
    return jnp.concatenate(rows, 0)


def project(rows, weight):
    return jnp.dot(rows, weight, preferred_element_type=jnp.float32).astype(jnp.bfloat16)


def body(
    latents,
    norm_gain,
    norm_bias,
    conv_weight,
    conv_bias,
    query_weight,
    key_weight,
    value_weight,
    out_weight,
    pos_table,
):
    frames, cells, width = latents.shape
    size = width // GROUPS
    devices = lax.axis_size("seq") * lax.axis_size("sub")
    place = place_of()
    own = latents[0]

    grouped = own.reshape(cells, GROUPS, size).astype(jnp.float32)
    partial = jnp.concatenate([jnp.sum(grouped, axis=(0, 2)), jnp.sum(grouped * grouped, axis=(0, 2))])
    stats = butterfly_sum(partial, devices)
    count = frames * devices * cells * size
    stats, pos_table, sent = lax.optimization_barrier((stats, pos_table, own))
    before = shifted(sent, devices, 1)
    before2 = shifted(sent, devices, 2)
    after = shifted(sent, devices, -1)
    wide = bias_table(pos_table)
    work = [(wide[h], head_bias) for h in range(wide.shape[0])]
    frame0, frame1, bias_all = broadcast_pair(sent, sent, place, devices, work)
    mean = stats[:GROUPS] / count
    meansq = stats[GROUPS:] / count
    inv = lax.rsqrt(meansq - mean * mean + EPS)
    mean_c = jnp.repeat(mean, size)
    inv_c = jnp.repeat(inv, size)

    def norm(x):
        return ((x.astype(jnp.float32) - mean_c) * inv_c * norm_gain + norm_bias).astype(jnp.bfloat16)

    zero = jnp.zeros((cells, width), jnp.bfloat16)
    n_self = norm(own)
    n_before = jnp.where(place >= 1, norm(before), zero)
    n_before2 = jnp.where(place >= 2, norm(before2), zero)
    n_after = jnp.where(place + 1 < devices, norm(after), zero)
    n_0 = norm(frame0)
    n_1 = norm(frame1)

    taps = [
        jnp.concatenate([n_before2, n_before], 0),
        jnp.concatenate([n_before, n_self], 0),
        jnp.concatenate([n_self, n_after], 0),
    ]
    acc = jnp.zeros((2 * cells, width), jnp.float32)
    for tap in range(3):
        acc = acc + jnp.dot(taps[tap], conv_weight[tap], preferred_element_type=jnp.float32)
    mixed = (taps[1].astype(jnp.float32) + acc + conv_bias).astype(jnp.bfloat16)
    mixed_prev = mixed[:cells]
    mixed_self = mixed[cells:]
    acc0 = jnp.dot(n_0, conv_weight[1], preferred_element_type=jnp.float32)
    acc0 = acc0 + jnp.dot(n_1, conv_weight[2], preferred_element_type=jnp.float32)
    mixed_first = (n_0.astype(jnp.float32) + acc0 + conv_bias).astype(jnp.bfloat16)

    queries = project(mixed_self, query_weight)
    first_key = project(mixed_first, key_weight)
    first_value = project(mixed_first, value_weight)
    leading = place <= 1
    prev_key = jnp.where(leading, first_key, project(mixed_prev, key_weight))
    prev_value = jnp.where(leading, first_value, project(mixed_prev, value_weight))

    scale = HEAD_DIM ** (-0.5)
    per_head = []
    for head in range(width // HEAD_DIM):
        cols = slice(head * HEAD_DIM, (head + 1) * HEAD_DIM)
        bias_head = bias_all[head]
        key_block = jnp.concatenate([first_key[:, cols], prev_key[:, cols]], 0)
        value_block = jnp.concatenate([first_value[:, cols], prev_value[:, cols]], 0)
        scores = jnp.dot(queries[:, cols], key_block.T, preferred_element_type=jnp.float32) * scale
        scores = (scores.reshape(cells, 2, cells) + bias_head[:, None, :]).reshape(cells, 2 * cells)
        peak = jnp.max(scores, axis=1, keepdims=True)
        weights = jnp.exp(scores - peak)
        probs = (weights / jnp.sum(weights, axis=1, keepdims=True)).astype(jnp.bfloat16)
        per_head.append(jnp.dot(probs, value_block, preferred_element_type=jnp.float32).astype(jnp.bfloat16))
    attended = jnp.concatenate(per_head, 1)
    result = own.astype(jnp.float32) + jnp.dot(attended, out_weight, preferred_element_type=jnp.float32)
    return result.astype(jnp.bfloat16).reshape(frames, cells, width)


def solution(mesh):
    return jax.shard_map(
        body,
        mesh=mesh,
        in_specs=(P(AXES, None, None), P(), P(), P(), P(), P(), P(), P(), P(), P()),
        out_specs=P(AXES, None, None),
        check_vma=False,
    )
```

```python
import numpy as np
import jax
import jax.numpy as jnp
from jax import lax
from jax.sharding import PartitionSpec as P

SIDE = 32
HEAD_DIM = 64
GROUPS = 32

EPS = 1e-05
AXES = ("seq", "sub")


def place_of():
    return lax.axis_index("seq") * lax.axis_size("sub") + lax.axis_index("sub")


def shifted(array, devices, by):
    pairs = [(i, i + by) for i in range(devices) if 0 <= i + by < devices]
    return lax.ppermute(array, AXES, pairs)


def butterfly_sum(x, devices):
    step = 1
    while step < devices:
        x = x + lax.ppermute(x, AXES, [(i, i ^ step) for i in range(devices)])
        step *= 2
    return x


def broadcast_pair(first, second, place, devices, work):
    step = 2
    done = []
    while step < devices:
        got_a = lax.ppermute(first, AXES, [(i, i + step) for i in range(0, step, 2)])
        got_b = lax.ppermute(second, AXES, [(i, i + step) for i in range(1, step, 2)])
        fresh = (place >= step) & (place < 2 * step)
        first = jnp.where(fresh & (place % 2 == 0), got_a, first)
        second = jnp.where(fresh & (place % 2 == 1), got_b, second)
        if len(done) < len(work):
            first, second, operand = lax.optimization_barrier((first, second, work[len(done)][0]))
            done.append(work[len(done)][1](operand))
        step *= 2
    swap_a = lax.ppermute(first, AXES, [(i, i ^ 1) for i in range(devices)])
    swap_b = lax.ppermute(second, AXES, [(i, i ^ 1) for i in range(devices)])
    even = place % 2 == 0
    return jnp.where(even, first, swap_a), jnp.where(even, swap_b, second), done


def bias_table(pos_table):
    heads, span, _ = pos_table.shape
    flipped = pos_table[:, ::-1, ::-1]
    coord = np.arange(SIDE)
    pick = np.arange(span)[:, None, None] == (SIDE - 1 - coord[:, None] + coord[None, :])[None]
    pick = jnp.asarray(pick.reshape(span, SIDE * SIDE), jnp.float32)
    table = jnp.einsum("hkj,jc->hkc", flipped, pick, precision=lax.Precision.HIGHEST)
    wide = jnp.transpose(table.reshape(heads, span, SIDE, SIDE), (0, 2, 1, 3))
    wide = wide.reshape(heads, SIDE, span * SIDE)
    return wide


def head_bias(wide_head):
    lanes = 128
    per = lanes // SIDE
    width = (SIDE - 1) // per * lanes + SIDE * SIDE
    shifted = [wide_head[:, SIDE * s : SIDE * s + width] for s in range(per)]
    rows = []
    for py in range(SIDE):
        start = (SIDE - 1 - py) * SIDE
        piece = shifted[start % lanes // SIDE]
        base = start // lanes * lanes
        rows.append(piece[:, base : base + SIDE * SIDE])
    return jnp.concatenate(rows, 0)


def project(rows, weight):
    return jnp.dot(rows, weight, preferred_element_type=jnp.float32).astype(jnp.bfloat16)


def body(
    latents,
    norm_gain,
    norm_bias,
    conv_weight,
    conv_bias,
    query_weight,
    key_weight,
    value_weight,
    out_weight,
    pos_table,
):
    frames, cells, width = latents.shape
    size = width // GROUPS
    devices = lax.axis_size("seq") * lax.axis_size("sub")
    place = place_of()
    own = latents[0]

    grouped = own.reshape(cells, GROUPS, size).astype(jnp.float32)
    partial = jnp.concatenate([jnp.sum(grouped, axis=(0, 2)), jnp.sum(grouped * grouped, axis=(0, 2))])
    stats = butterfly_sum(partial, devices)
    count = frames * devices * cells * size
    stats, pos_table, sent = lax.optimization_barrier((stats, pos_table, own))
    before = shifted(sent, devices, 1)
    before2 = shifted(sent, devices, 2)
    after = shifted(sent, devices, -1)
    wide = bias_table(pos_table)
    work = [(wide[h], head_bias) for h in range(wide.shape[0])]
    frame0, frame1, bias_all = broadcast_pair(sent, sent, place, devices, work)
    mean = stats[:GROUPS] / count
    meansq = stats[GROUPS:] / count
    inv = lax.rsqrt(meansq - mean * mean + EPS)
    mean_c = jnp.repeat(mean, size)
    inv_c = jnp.repeat(inv, size)

    def norm(x):
        return ((x.astype(jnp.float32) - mean_c) * inv_c * norm_gain + norm_bias).astype(jnp.bfloat16)

    zero = jnp.zeros((cells, width), jnp.bfloat16)
    n_self = norm(own)
    n_before = jnp.where(place >= 1, norm(before), zero)
    n_before2 = jnp.where(place >= 2, norm(before2), zero)
    n_after = jnp.where(place + 1 < devices, norm(after), zero)
    n_0 = norm(frame0)
    n_1 = norm(frame1)

    taps = [
        jnp.concatenate([n_before2, n_before], 0),
        jnp.concatenate([n_before, n_self], 0),
        jnp.concatenate([n_self, n_after], 0),
    ]
    acc = jnp.zeros((2 * cells, width), jnp.float32)
    for tap in range(3):
        acc = acc + jnp.dot(taps[tap], conv_weight[tap], preferred_element_type=jnp.float32)
    mixed = (taps[1].astype(jnp.float32) + acc + conv_bias).astype(jnp.bfloat16)
    mixed_prev = mixed[:cells]
    mixed_self = mixed[cells:]
    acc0 = jnp.dot(n_0, conv_weight[1], preferred_element_type=jnp.float32)
    acc0 = acc0 + jnp.dot(n_1, conv_weight[2], preferred_element_type=jnp.float32)
    mixed_first = (n_0.astype(jnp.float32) + acc0 + conv_bias).astype(jnp.bfloat16)

    queries = project(mixed_self, query_weight)
    first_key = project(mixed_first, key_weight)
    first_value = project(mixed_first, value_weight)
    leading = place <= 1
    prev_key = jnp.where(leading, first_key, project(mixed_prev, key_weight))
    prev_value = jnp.where(leading, first_value, project(mixed_prev, value_weight))

    scale = HEAD_DIM ** (-0.5)
    per_head = []

    def block(query, key, value, bias):
        scores = jnp.dot(query, key.T, preferred_element_type=jnp.float32) * scale + bias
        peak = jnp.max(scores, axis=1, keepdims=True)
        weights = jnp.exp(scores - peak)
        total = jnp.sum(weights, axis=1, keepdims=True)
        out = jnp.dot(weights.astype(jnp.bfloat16), value, preferred_element_type=jnp.float32)
        return peak, total, out

    for head in range(width // HEAD_DIM):
        cols = slice(head * HEAD_DIM, (head + 1) * HEAD_DIM)
        bias_head = bias_all[head]
        query = queries[:, cols]
        peak_p, total_p, out_p = block(query, prev_key[:, cols], prev_value[:, cols], bias_head)
        peak_f, total_f, out_f = block(query, first_key[:, cols], first_value[:, cols], bias_head)
        peak = jnp.maximum(peak_p, peak_f)
        scale_p = jnp.exp(peak_p - peak)
        scale_f = jnp.exp(peak_f - peak)
        total = total_p * scale_p + total_f * scale_f
        out = (out_p * scale_p + out_f * scale_f) / total
        per_head.append(out.astype(jnp.bfloat16))
    attended = jnp.concatenate(per_head, 1)
    result = own.astype(jnp.float32) + jnp.dot(attended, out_weight, preferred_element_type=jnp.float32)
    return result.astype(jnp.bfloat16).reshape(frames, cells, width)


def solution(mesh):
    return jax.shard_map(
        body,
        mesh=mesh,
        in_specs=(P(AXES, None, None), P(), P(), P(), P(), P(), P(), P(), P(), P()),
        out_specs=P(AXES, None, None),
        check_vma=False,
    )
```

```python
import numpy as np
import jax
import jax.numpy as jnp
from jax import lax
from jax.sharding import PartitionSpec as P

SIDE = 32
HEAD_DIM = 64
GROUPS = 32

EPS = 1e-05
AXES = ("seq", "sub")


def place_of():
    return lax.axis_index("seq") * lax.axis_size("sub") + lax.axis_index("sub")


def shifted(array, devices, by):
    pairs = [(i, i + by) for i in range(devices) if 0 <= i + by < devices]
    return lax.ppermute(array, AXES, pairs)


def butterfly_sum(x, devices):
    step = 1
    while step < devices:
        x = x + lax.ppermute(x, AXES, [(i, i ^ step) for i in range(devices)])
        step *= 2
    return x


def halves(array, pairs):
    middle = array.shape[0] // 2
    low = lax.ppermute(array[:middle], AXES, pairs)
    high = lax.ppermute(array[middle:], AXES, pairs)
    return jnp.concatenate([low, high], 0)


def broadcast_pair(first, second, place, devices, work):
    step = 2
    done = []
    while step < devices:
        got_a = halves(first, [(i, i + step) for i in range(0, step, 2)])
        got_b = halves(second, [(i, i + step) for i in range(1, step, 2)])
        fresh = (place >= step) & (place < 2 * step)
        first = jnp.where(fresh & (place % 2 == 0), got_a, first)
        second = jnp.where(fresh & (place % 2 == 1), got_b, second)
        if len(done) < len(work):
            first, second, operand = lax.optimization_barrier((first, second, work[len(done)][0]))
            done.append(work[len(done)][1](operand))
        step *= 2
    swap_a = halves(first, [(i, i ^ 1) for i in range(devices)])
    swap_b = halves(second, [(i, i ^ 1) for i in range(devices)])
    even = place % 2 == 0
    return jnp.where(even, first, swap_a), jnp.where(even, swap_b, second), done


def bias_table(pos_table):
    heads, span, _ = pos_table.shape
    flipped = pos_table[:, ::-1, ::-1]
    coord = np.arange(SIDE)
    pick = np.arange(span)[:, None, None] == (SIDE - 1 - coord[:, None] + coord[None, :])[None]
    pick = jnp.asarray(pick.reshape(span, SIDE * SIDE), jnp.float32)
    table = jnp.einsum("hkj,jc->hkc", flipped, pick, precision=lax.Precision.HIGHEST)
    wide = jnp.transpose(table.reshape(heads, span, SIDE, SIDE), (0, 2, 1, 3))
    wide = wide.reshape(heads, SIDE, span * SIDE)
    return wide


def head_bias(wide_head):
    lanes = 128
    per = lanes // SIDE
    width = (SIDE - 1) // per * lanes + SIDE * SIDE
    shifted = [wide_head[:, SIDE * s : SIDE * s + width] for s in range(per)]
    rows = []
    for py in range(SIDE):
        start = (SIDE - 1 - py) * SIDE
        piece = shifted[start % lanes // SIDE]
        base = start // lanes * lanes
        rows.append(piece[:, base : base + SIDE * SIDE])
    return jnp.concatenate(rows, 0)


def project(rows, weight):
    return jnp.dot(rows, weight, preferred_element_type=jnp.float32).astype(jnp.bfloat16)


def body(
    latents,
    norm_gain,
    norm_bias,
    conv_weight,
    conv_bias,
    query_weight,
    key_weight,
    value_weight,
    out_weight,
    pos_table,
):
    frames, cells, width = latents.shape
    size = width // GROUPS
    devices = lax.axis_size("seq") * lax.axis_size("sub")
    place = place_of()
    own = latents[0]

    grouped = own.reshape(cells, GROUPS, size).astype(jnp.float32)
    partial = jnp.concatenate([jnp.sum(grouped, axis=(0, 2)), jnp.sum(grouped * grouped, axis=(0, 2))])
    stats = butterfly_sum(partial, devices)
    count = frames * devices * cells * size
    stats, pos_table, sent = lax.optimization_barrier((stats, pos_table, own))
    before = shifted(sent, devices, 1)
    before2 = shifted(sent, devices, 2)
    after = shifted(sent, devices, -1)
    wide = bias_table(pos_table)
    work = [(wide[h], head_bias) for h in range(wide.shape[0])]
    frame0, frame1, bias_all = broadcast_pair(sent, sent, place, devices, work)
    mean = stats[:GROUPS] / count
    meansq = stats[GROUPS:] / count
    inv = lax.rsqrt(meansq - mean * mean + EPS)
    mean_c = jnp.repeat(mean, size)
    inv_c = jnp.repeat(inv, size)

    def norm(x):
        return ((x.astype(jnp.float32) - mean_c) * inv_c * norm_gain + norm_bias).astype(jnp.bfloat16)

    zero = jnp.zeros((cells, width), jnp.bfloat16)
    n_self = norm(own)
    n_before = jnp.where(place >= 1, norm(before), zero)
    n_before2 = jnp.where(place >= 2, norm(before2), zero)
    n_after = jnp.where(place + 1 < devices, norm(after), zero)
    n_0 = norm(frame0)
    n_1 = norm(frame1)

    taps = [
        jnp.concatenate([n_before2, n_before], 0),
        jnp.concatenate([n_before, n_self], 0),
        jnp.concatenate([n_self, n_after], 0),
    ]
    acc = jnp.zeros((2 * cells, width), jnp.float32)
    for tap in range(3):
        acc = acc + jnp.dot(taps[tap], conv_weight[tap], preferred_element_type=jnp.float32)
    mixed = (taps[1].astype(jnp.float32) + acc + conv_bias).astype(jnp.bfloat16)
    mixed_prev = mixed[:cells]
    mixed_self = mixed[cells:]
    acc0 = jnp.dot(n_0, conv_weight[1], preferred_element_type=jnp.float32)
    acc0 = acc0 + jnp.dot(n_1, conv_weight[2], preferred_element_type=jnp.float32)
    mixed_first = (n_0.astype(jnp.float32) + acc0 + conv_bias).astype(jnp.bfloat16)

    queries = project(mixed_self, query_weight)
    first_key = project(mixed_first, key_weight)
    first_value = project(mixed_first, value_weight)
    leading = place <= 1
    prev_key = jnp.where(leading, first_key, project(mixed_prev, key_weight))
    prev_value = jnp.where(leading, first_value, project(mixed_prev, value_weight))

    scale = HEAD_DIM ** (-0.5)
    per_head = []
    for head in range(width // HEAD_DIM):
        cols = slice(head * HEAD_DIM, (head + 1) * HEAD_DIM)
        bias_head = bias_all[head]
        key_block = jnp.concatenate([first_key[:, cols], prev_key[:, cols]], 0)
        value_block = jnp.concatenate([first_value[:, cols], prev_value[:, cols]], 0)
        scores = jnp.dot(queries[:, cols], key_block.T, preferred_element_type=jnp.float32) * scale
        scores = (scores.reshape(cells, 2, cells) + bias_head[:, None, :]).reshape(cells, 2 * cells)
        peak = jnp.max(scores, axis=1, keepdims=True)
        weights = jnp.exp(scores - peak)
        probs = (weights / jnp.sum(weights, axis=1, keepdims=True)).astype(jnp.bfloat16)
        per_head.append(jnp.dot(probs, value_block, preferred_element_type=jnp.float32).astype(jnp.bfloat16))
    attended = jnp.concatenate(per_head, 1)
    result = own.astype(jnp.float32) + jnp.dot(attended, out_weight, preferred_element_type=jnp.float32)
    return result.astype(jnp.bfloat16).reshape(frames, cells, width)


def solution(mesh):
    return jax.shard_map(
        body,
        mesh=mesh,
        in_specs=(P(AXES, None, None), P(), P(), P(), P(), P(), P(), P(), P(), P()),
        out_specs=P(AXES, None, None),
        check_vma=False,
    )
```

```python
import numpy as np
import jax
import jax.numpy as jnp
from jax import lax
from jax.sharding import PartitionSpec as P

SIDE = 32
HEAD_DIM = 64
GROUPS = 32

EPS = 1e-05
AXES = ("seq", "sub")


def place_of():
    return lax.axis_index("seq") * lax.axis_size("sub") + lax.axis_index("sub")


def shifted(array, devices, by):
    pairs = [(i, i + by) for i in range(devices) if 0 <= i + by < devices]
    return lax.ppermute(array, AXES, pairs)


def butterfly_sum(x, devices):
    step = 1
    while step < devices:
        x = x + lax.ppermute(x, AXES, [(i, i ^ step) for i in range(devices)])
        step *= 2
    return x


def broadcast_pair(first, second, place, devices, work):
    holders = 1
    trees = devices // 2
    done = []
    rounds = 0
    while holders < trees:
        for t in range(1, 4):
            pairs = [(j, j + t * holders) for j in range(holders) if j + t * holders < trees]
            got_a = lax.ppermute(first, AXES, [(2 * a, 2 * b) for a, b in pairs])
            got_b = lax.ppermute(second, AXES, [(2 * a + 1, 2 * b + 1) for a, b in pairs])
            fresh = (place // 2 >= t * holders) & (place // 2 < (t + 1) * holders)
            first = jnp.where(fresh & (place % 2 == 0), got_a, first)
            second = jnp.where(fresh & (place % 2 == 1), got_b, second)
        if rounds < len(work):
            first, second, operands = lax.optimization_barrier((first, second, [w[0] for w in work[rounds]]))
            done.extend(w[1](o) for w, o in zip(work[rounds], operands))
        rounds += 1
        holders *= 4
    for items in work[rounds:]:
        done.extend(w[1](w[0]) for w in items)
    swap_a = lax.ppermute(first, AXES, [(i, i ^ 1) for i in range(devices)])
    swap_b = lax.ppermute(second, AXES, [(i, i ^ 1) for i in range(devices)])
    even = place % 2 == 0
    return jnp.where(even, first, swap_a), jnp.where(even, swap_b, second), done


def bias_table(pos_table):
    heads, span, _ = pos_table.shape
    flipped = pos_table[:, ::-1, ::-1]
    coord = np.arange(SIDE)
    pick = np.arange(span)[:, None, None] == (SIDE - 1 - coord[:, None] + coord[None, :])[None]
    pick = jnp.asarray(pick.reshape(span, SIDE * SIDE), jnp.float32)
    table = jnp.einsum("hkj,jc->hkc", flipped, pick, precision=lax.Precision.HIGHEST)
    wide = jnp.transpose(table.reshape(heads, span, SIDE, SIDE), (0, 2, 1, 3))
    wide = wide.reshape(heads, SIDE, span * SIDE)
    return wide


def head_bias(wide_head):
    lanes = 128
    per = lanes // SIDE
    width = (SIDE - 1) // per * lanes + SIDE * SIDE
    shifted = [wide_head[:, SIDE * s : SIDE * s + width] for s in range(per)]
    rows = []
    for py in range(SIDE):
        start = (SIDE - 1 - py) * SIDE
        piece = shifted[start % lanes // SIDE]
        base = start // lanes * lanes
        rows.append(piece[:, base : base + SIDE * SIDE])
    return jnp.concatenate(rows, 0)


def project(rows, weight):
    return jnp.dot(rows, weight, preferred_element_type=jnp.float32).astype(jnp.bfloat16)


def body(
    latents,
    norm_gain,
    norm_bias,
    conv_weight,
    conv_bias,
    query_weight,
    key_weight,
    value_weight,
    out_weight,
    pos_table,
):
    frames, cells, width = latents.shape
    size = width // GROUPS
    devices = lax.axis_size("seq") * lax.axis_size("sub")
    place = place_of()
    own = latents[0]

    grouped = own.reshape(cells, GROUPS, size).astype(jnp.float32)
    partial = jnp.concatenate([jnp.sum(grouped, axis=(0, 2)), jnp.sum(grouped * grouped, axis=(0, 2))])
    stats = butterfly_sum(partial, devices)
    count = frames * devices * cells * size
    stats, pos_table, sent = lax.optimization_barrier((stats, pos_table, own))
    before = shifted(sent, devices, 1)
    before2 = shifted(sent, devices, 2)
    after = shifted(sent, devices, -1)
    wide = bias_table(pos_table)
    work = [[(wide[h], head_bias) for h in group] for group in ((0, 1), (2, 3), (4,))]
    frame0, frame1, bias_all = broadcast_pair(sent, sent, place, devices, work)
    mean = stats[:GROUPS] / count
    meansq = stats[GROUPS:] / count
    inv = lax.rsqrt(meansq - mean * mean + EPS)
    mean_c = jnp.repeat(mean, size)
    inv_c = jnp.repeat(inv, size)

    def norm(x):
        return ((x.astype(jnp.float32) - mean_c) * inv_c * norm_gain + norm_bias).astype(jnp.bfloat16)

    zero = jnp.zeros((cells, width), jnp.bfloat16)
    n_self = norm(own)
    n_before = jnp.where(place >= 1, norm(before), zero)
    n_before2 = jnp.where(place >= 2, norm(before2), zero)
    n_after = jnp.where(place + 1 < devices, norm(after), zero)
    n_0 = norm(frame0)
    n_1 = norm(frame1)

    taps = [
        jnp.concatenate([n_before2, n_before], 0),
        jnp.concatenate([n_before, n_self], 0),
        jnp.concatenate([n_self, n_after], 0),
    ]
    acc = jnp.zeros((2 * cells, width), jnp.float32)
    for tap in range(3):
        acc = acc + jnp.dot(taps[tap], conv_weight[tap], preferred_element_type=jnp.float32)
    mixed = (taps[1].astype(jnp.float32) + acc + conv_bias).astype(jnp.bfloat16)
    mixed_prev = mixed[:cells]
    mixed_self = mixed[cells:]
    acc0 = jnp.dot(n_0, conv_weight[1], preferred_element_type=jnp.float32)
    acc0 = acc0 + jnp.dot(n_1, conv_weight[2], preferred_element_type=jnp.float32)
    mixed_first = (n_0.astype(jnp.float32) + acc0 + conv_bias).astype(jnp.bfloat16)

    queries = project(mixed_self, query_weight)
    first_key = project(mixed_first, key_weight)
    first_value = project(mixed_first, value_weight)
    leading = place <= 1
    prev_key = jnp.where(leading, first_key, project(mixed_prev, key_weight))
    prev_value = jnp.where(leading, first_value, project(mixed_prev, value_weight))

    scale = HEAD_DIM ** (-0.5)
    per_head = []
    for head in range(width // HEAD_DIM):
        cols = slice(head * HEAD_DIM, (head + 1) * HEAD_DIM)
        bias_head = bias_all[head]
        key_block = jnp.concatenate([first_key[:, cols], prev_key[:, cols]], 0)
        value_block = jnp.concatenate([first_value[:, cols], prev_value[:, cols]], 0)
        scores = jnp.dot(queries[:, cols], key_block.T, preferred_element_type=jnp.float32) * scale
        scores = (scores.reshape(cells, 2, cells) + bias_head[:, None, :]).reshape(cells, 2 * cells)
        peak = jnp.max(scores, axis=1, keepdims=True)
        weights = jnp.exp(scores - peak)
        probs = (weights / jnp.sum(weights, axis=1, keepdims=True)).astype(jnp.bfloat16)
        per_head.append(jnp.dot(probs, value_block, preferred_element_type=jnp.float32).astype(jnp.bfloat16))
    attended = jnp.concatenate(per_head, 1)
    result = own.astype(jnp.float32) + jnp.dot(attended, out_weight, preferred_element_type=jnp.float32)
    return result.astype(jnp.bfloat16).reshape(frames, cells, width)


def solution(mesh):
    return jax.shard_map(
        body,
        mesh=mesh,
        in_specs=(P(AXES, None, None), P(), P(), P(), P(), P(), P(), P(), P(), P()),
        out_specs=P(AXES, None, None),
        check_vma=False,
    )
```

```python
import numpy as np
import jax
import jax.numpy as jnp
from jax import lax
from jax.sharding import PartitionSpec as P

SIDE = 32
HEAD_DIM = 64
GROUPS = 32

EPS = 1e-05
AXES = ("seq", "sub")


def place_of():
    return lax.axis_index("seq") * lax.axis_size("sub") + lax.axis_index("sub")


def shifted(array, devices, by):
    pairs = [(i, i + by) for i in range(devices) if 0 <= i + by < devices]
    return lax.ppermute(array, AXES, pairs)


def butterfly_sum(x, devices):
    step = 1
    while step < devices:
        x = x + lax.ppermute(x, AXES, [(i, i ^ step) for i in range(devices)])
        step *= 2
    return x


def broadcast_pair(first, second, place, devices, work):
    holders = 1
    trees = devices // 2
    done = []
    rounds = 0
    while holders < trees:
        sources = (first, second)
        for t in range(1, 4):
            pairs = [(j, j + t * holders) for j in range(holders) if j + t * holders < trees]
            got_a = lax.ppermute(sources[0], AXES, [(2 * a, 2 * b) for a, b in pairs])
            got_b = lax.ppermute(sources[1], AXES, [(2 * a + 1, 2 * b + 1) for a, b in pairs])
            fresh = (place // 2 >= t * holders) & (place // 2 < (t + 1) * holders)
            first = jnp.where(fresh & (place % 2 == 0), got_a, first)
            second = jnp.where(fresh & (place % 2 == 1), got_b, second)
        if rounds < len(work):
            first, second, operands = lax.optimization_barrier((first, second, [w[0] for w in work[rounds]]))
            done.extend(w[1](o) for w, o in zip(work[rounds], operands))
        rounds += 1
        holders *= 4
    for items in work[rounds:]:
        done.extend(w[1](w[0]) for w in items)
    swap_a = lax.ppermute(first, AXES, [(i, i ^ 1) for i in range(devices)])
    swap_b = lax.ppermute(second, AXES, [(i, i ^ 1) for i in range(devices)])
    even = place % 2 == 0
    return jnp.where(even, first, swap_a), jnp.where(even, swap_b, second), done


def bias_table(pos_table):
    heads, span, _ = pos_table.shape
    flipped = pos_table[:, ::-1, ::-1]
    coord = np.arange(SIDE)
    pick = np.arange(span)[:, None, None] == (SIDE - 1 - coord[:, None] + coord[None, :])[None]
    pick = jnp.asarray(pick.reshape(span, SIDE * SIDE), jnp.float32)
    table = jnp.einsum("hkj,jc->hkc", flipped, pick, precision=lax.Precision.HIGHEST)
    wide = jnp.transpose(table.reshape(heads, span, SIDE, SIDE), (0, 2, 1, 3))
    wide = wide.reshape(heads, SIDE, span * SIDE)
    return wide


def head_bias(wide_head):
    lanes = 128
    per = lanes // SIDE
    width = (SIDE - 1) // per * lanes + SIDE * SIDE
    shifted = [wide_head[:, SIDE * s : SIDE * s + width] for s in range(per)]
    rows = []
    for py in range(SIDE):
        start = (SIDE - 1 - py) * SIDE
        piece = shifted[start % lanes // SIDE]
        base = start // lanes * lanes
        rows.append(piece[:, base : base + SIDE * SIDE])
    return jnp.concatenate(rows, 0)


def project(rows, weight):
    return jnp.dot(rows, weight, preferred_element_type=jnp.float32).astype(jnp.bfloat16)


def body(
    latents,
    norm_gain,
    norm_bias,
    conv_weight,
    conv_bias,
    query_weight,
    key_weight,
    value_weight,
    out_weight,
    pos_table,
):
    frames, cells, width = latents.shape
    size = width // GROUPS
    devices = lax.axis_size("seq") * lax.axis_size("sub")
    place = place_of()
    own = latents[0]

    grouped = own.reshape(cells, GROUPS, size).astype(jnp.float32)
    partial = jnp.concatenate([jnp.sum(grouped, axis=(0, 2)), jnp.sum(grouped * grouped, axis=(0, 2))])
    stats = butterfly_sum(partial, devices)
    count = frames * devices * cells * size
    stats, pos_table, sent = lax.optimization_barrier((stats, pos_table, own))
    before = shifted(sent, devices, 1)
    before2 = shifted(sent, devices, 2)
    after = shifted(sent, devices, -1)
    wide = bias_table(pos_table)
    work = [[(wide[h], head_bias) for h in group] for group in ((0, 1), (2, 3), (4,))]
    frame0, frame1, bias_all = broadcast_pair(sent, sent, place, devices, work)
    mean = stats[:GROUPS] / count
    meansq = stats[GROUPS:] / count
    inv = lax.rsqrt(meansq - mean * mean + EPS)
    mean_c = jnp.repeat(mean, size)
    inv_c = jnp.repeat(inv, size)

    def norm(x):
        return ((x.astype(jnp.float32) - mean_c) * inv_c * norm_gain + norm_bias).astype(jnp.bfloat16)

    zero = jnp.zeros((cells, width), jnp.bfloat16)
    n_self = norm(own)
    n_before = jnp.where(place >= 1, norm(before), zero)
    n_before2 = jnp.where(place >= 2, norm(before2), zero)
    n_after = jnp.where(place + 1 < devices, norm(after), zero)
    n_0 = norm(frame0)
    n_1 = norm(frame1)

    taps = [
        jnp.concatenate([n_before2, n_before], 0),
        jnp.concatenate([n_before, n_self], 0),
        jnp.concatenate([n_self, n_after], 0),
    ]
    acc = jnp.zeros((2 * cells, width), jnp.float32)
    for tap in range(3):
        acc = acc + jnp.dot(taps[tap], conv_weight[tap], preferred_element_type=jnp.float32)
    mixed = (taps[1].astype(jnp.float32) + acc + conv_bias).astype(jnp.bfloat16)
    mixed_prev = mixed[:cells]
    mixed_self = mixed[cells:]
    acc0 = jnp.dot(n_0, conv_weight[1], preferred_element_type=jnp.float32)
    acc0 = acc0 + jnp.dot(n_1, conv_weight[2], preferred_element_type=jnp.float32)
    mixed_first = (n_0.astype(jnp.float32) + acc0 + conv_bias).astype(jnp.bfloat16)

    queries = project(mixed_self, query_weight)
    first_key = project(mixed_first, key_weight)
    first_value = project(mixed_first, value_weight)
    leading = place <= 1
    prev_key = jnp.where(leading, first_key, project(mixed_prev, key_weight))
    prev_value = jnp.where(leading, first_value, project(mixed_prev, value_weight))

    scale = HEAD_DIM ** (-0.5)
    per_head = []
    for head in range(width // HEAD_DIM):
        cols = slice(head * HEAD_DIM, (head + 1) * HEAD_DIM)
        bias_head = bias_all[head]
        key_block = jnp.concatenate([first_key[:, cols], prev_key[:, cols]], 0)
        value_block = jnp.concatenate([first_value[:, cols], prev_value[:, cols]], 0)
        scores = jnp.dot(queries[:, cols], key_block.T, preferred_element_type=jnp.float32) * scale
        scores = (scores.reshape(cells, 2, cells) + bias_head[:, None, :]).reshape(cells, 2 * cells)
        peak = jnp.max(scores, axis=1, keepdims=True)
        weights = jnp.exp(scores - peak)
        probs = (weights / jnp.sum(weights, axis=1, keepdims=True)).astype(jnp.bfloat16)
        per_head.append(jnp.dot(probs, value_block, preferred_element_type=jnp.float32).astype(jnp.bfloat16))
    attended = jnp.concatenate(per_head, 1)
    result = own.astype(jnp.float32) + jnp.dot(attended, out_weight, preferred_element_type=jnp.float32)
    return result.astype(jnp.bfloat16).reshape(frames, cells, width)


def solution(mesh):
    return jax.shard_map(
        body,
        mesh=mesh,
        in_specs=(P(AXES, None, None), P(), P(), P(), P(), P(), P(), P(), P(), P()),
        out_specs=P(AXES, None, None),
        check_vma=False,
    )
```

```python
import numpy as np
import jax
import jax.numpy as jnp
from jax import lax
from jax.sharding import PartitionSpec as P

SIDE = 32
HEAD_DIM = 64
GROUPS = 32

EPS = 1e-05
AXES = ("seq", "sub")


def place_of():
    return lax.axis_index("seq") * lax.axis_size("sub") + lax.axis_index("sub")


def shifted(array, devices, by):
    pairs = [(i, i + by) for i in range(devices) if 0 <= i + by < devices]
    return lax.ppermute(array, AXES, pairs)


def butterfly_sum(x, devices):
    step = 1
    while step < devices:
        x = x + lax.ppermute(x, AXES, [(i, i ^ step) for i in range(devices)])
        step *= 2
    return x


def broadcast_pair(first, second, place, devices, work):
    step = 2
    done = []
    rounds = 0
    while step < devices:
        got_a = lax.ppermute(first, AXES, [(i, i + step) for i in range(0, step, 2)])
        got_b = lax.ppermute(second, AXES, [(i, i + step) for i in range(1, step, 2)])
        fresh = (place >= step) & (place < 2 * step)
        first = jnp.where(fresh & (place % 2 == 0), got_a, first)
        second = jnp.where(fresh & (place % 2 == 1), got_b, second)
        if rounds < len(work) and work[rounds] is not None:
            first, second, operand = lax.optimization_barrier((first, second, work[rounds][0]))
            done.append(work[rounds][1](operand))
        rounds += 1
        step *= 2
    for item in work[rounds:]:
        done.append(item[1](item[0]))
    swap_a = lax.ppermute(first, AXES, [(i, i ^ 1) for i in range(devices)])
    swap_b = lax.ppermute(second, AXES, [(i, i ^ 1) for i in range(devices)])
    even = place % 2 == 0
    return jnp.where(even, first, swap_a), jnp.where(even, swap_b, second), done


def bias_table(pos_table):
    heads, span, _ = pos_table.shape
    flipped = pos_table[:, ::-1, ::-1]
    coord = np.arange(SIDE)
    pick = np.arange(span)[:, None, None] == (SIDE - 1 - coord[:, None] + coord[None, :])[None]
    pick = jnp.asarray(pick.reshape(span, SIDE * SIDE), jnp.float32)
    table = jnp.einsum("hkj,jc->hkc", flipped, pick, precision=lax.Precision.HIGHEST)
    wide = jnp.transpose(table.reshape(heads, span, SIDE, SIDE), (0, 2, 1, 3))
    wide = wide.reshape(heads, SIDE, span * SIDE)
    return wide


def head_bias(wide_head):
    lanes = 128
    per = lanes // SIDE
    width = (SIDE - 1) // per * lanes + SIDE * SIDE
    shifted = [wide_head[:, SIDE * s : SIDE * s + width] for s in range(per)]
    rows = []
    for py in range(SIDE):
        start = (SIDE - 1 - py) * SIDE
        piece = shifted[start % lanes // SIDE]
        base = start // lanes * lanes
        rows.append(piece[:, base : base + SIDE * SIDE])
    return jnp.concatenate(rows, 0)


def project(rows, weight):
    return jnp.dot(rows, weight, preferred_element_type=jnp.float32).astype(jnp.bfloat16)


def body(
    latents,
    norm_gain,
    norm_bias,
    conv_weight,
    conv_bias,
    query_weight,
    key_weight,
    value_weight,
    out_weight,
    pos_table,
):
    frames, cells, width = latents.shape
    size = width // GROUPS
    devices = lax.axis_size("seq") * lax.axis_size("sub")
    place = place_of()
    own = latents[0]

    grouped = own.reshape(cells, GROUPS, size).astype(jnp.float32)
    partial = jnp.concatenate([jnp.sum(grouped, axis=(0, 2)), jnp.sum(grouped * grouped, axis=(0, 2))])
    stats = butterfly_sum(partial, devices)
    count = frames * devices * cells * size
    stats, pos_table, sent = lax.optimization_barrier((stats, pos_table, own))
    before = shifted(sent, devices, 1)
    before2 = shifted(sent, devices, 2)
    after = shifted(sent, devices, -1)
    wide = bias_table(pos_table)
    work = [(wide[h], head_bias) for h in range(wide.shape[0])]
    frame0, frame1, bias_all = broadcast_pair(own, own, place, devices, [None] + work)
    mean = stats[:GROUPS] / count
    meansq = stats[GROUPS:] / count
    inv = lax.rsqrt(meansq - mean * mean + EPS)
    mean_c = jnp.repeat(mean, size)
    inv_c = jnp.repeat(inv, size)

    def norm(x):
        return ((x.astype(jnp.float32) - mean_c) * inv_c * norm_gain + norm_bias).astype(jnp.bfloat16)

    zero = jnp.zeros((cells, width), jnp.bfloat16)
    n_self = norm(own)
    n_before = jnp.where(place >= 1, norm(before), zero)
    n_before2 = jnp.where(place >= 2, norm(before2), zero)
    n_after = jnp.where(place + 1 < devices, norm(after), zero)
    n_0 = norm(frame0)
    n_1 = norm(frame1)

    taps = [
        jnp.concatenate([n_before2, n_before], 0),
        jnp.concatenate([n_before, n_self], 0),
        jnp.concatenate([n_self, n_after], 0),
    ]
    acc = jnp.zeros((2 * cells, width), jnp.float32)
    for tap in range(3):
        acc = acc + jnp.dot(taps[tap], conv_weight[tap], preferred_element_type=jnp.float32)
    mixed = (taps[1].astype(jnp.float32) + acc + conv_bias).astype(jnp.bfloat16)
    mixed_prev = mixed[:cells]
    mixed_self = mixed[cells:]
    acc0 = jnp.dot(n_0, conv_weight[1], preferred_element_type=jnp.float32)
    acc0 = acc0 + jnp.dot(n_1, conv_weight[2], preferred_element_type=jnp.float32)
    mixed_first = (n_0.astype(jnp.float32) + acc0 + conv_bias).astype(jnp.bfloat16)

    queries = project(mixed_self, query_weight)
    first_key = project(mixed_first, key_weight)
    first_value = project(mixed_first, value_weight)
    leading = place <= 1
    prev_key = jnp.where(leading, first_key, project(mixed_prev, key_weight))
    prev_value = jnp.where(leading, first_value, project(mixed_prev, value_weight))

    scale = HEAD_DIM ** (-0.5)
    per_head = []
    for head in range(width // HEAD_DIM):
        cols = slice(head * HEAD_DIM, (head + 1) * HEAD_DIM)
        bias_head = bias_all[head]
        key_block = jnp.concatenate([first_key[:, cols], prev_key[:, cols]], 0)
        value_block = jnp.concatenate([first_value[:, cols], prev_value[:, cols]], 0)
        scores = jnp.dot(queries[:, cols], key_block.T, preferred_element_type=jnp.float32) * scale
        scores = (scores.reshape(cells, 2, cells) + bias_head[:, None, :]).reshape(cells, 2 * cells)
        peak = jnp.max(scores, axis=1, keepdims=True)
        weights = jnp.exp(scores - peak)
        probs = (weights / jnp.sum(weights, axis=1, keepdims=True)).astype(jnp.bfloat16)
        per_head.append(jnp.dot(probs, value_block, preferred_element_type=jnp.float32).astype(jnp.bfloat16))
    attended = jnp.concatenate(per_head, 1)
    result = own.astype(jnp.float32) + jnp.dot(attended, out_weight, preferred_element_type=jnp.float32)
    return result.astype(jnp.bfloat16).reshape(frames, cells, width)


def solution(mesh):
    return jax.shard_map(
        body,
        mesh=mesh,
        in_specs=(P(AXES, None, None), P(), P(), P(), P(), P(), P(), P(), P(), P()),
        out_specs=P(AXES, None, None),
        check_vma=False,
    )
```

```python
import numpy as np
import jax
import jax.numpy as jnp
from jax import lax
from jax.sharding import PartitionSpec as P

SIDE = 32
HEAD_DIM = 64
GROUPS = 32

EPS = 1e-05
AXES = ("seq", "sub")


def place_of():
    return lax.axis_index("seq") * lax.axis_size("sub") + lax.axis_index("sub")


def shifted(array, devices, by):
    pairs = [(i, i + by) for i in range(devices) if 0 <= i + by < devices]
    return lax.ppermute(array, AXES, pairs)


def butterfly_sum(x, devices, tied, tie_at):
    step = 1
    while step < devices:
        if step == tie_at:
            x, tied = lax.optimization_barrier((x, tied))
        x = x + lax.ppermute(x, AXES, [(i, i ^ step) for i in range(devices)])
        step *= 2
    return x, tied


def broadcast_pair(first, second, place, devices, work, step=2):
    done = []
    rounds = 0
    while step < devices:
        got_a = lax.ppermute(first, AXES, [(i, i + step) for i in range(0, step, 2)])
        got_b = lax.ppermute(second, AXES, [(i, i + step) for i in range(1, step, 2)])
        fresh = (place >= step) & (place < 2 * step)
        first = jnp.where(fresh & (place % 2 == 0), got_a, first)
        second = jnp.where(fresh & (place % 2 == 1), got_b, second)
        if rounds < len(work) and work[rounds] is not None:
            first, second, operand = lax.optimization_barrier((first, second, work[rounds][0]))
            done.append(work[rounds][1](operand))
        rounds += 1
        step *= 2
    for item in work[rounds:]:
        done.append(item[1](item[0]))
    swap_a = lax.ppermute(first, AXES, [(i, i ^ 1) for i in range(devices)])
    swap_b = lax.ppermute(second, AXES, [(i, i ^ 1) for i in range(devices)])
    even = place % 2 == 0
    return jnp.where(even, first, swap_a), jnp.where(even, swap_b, second), done


def bias_table(pos_table):
    heads, span, _ = pos_table.shape
    flipped = pos_table[:, ::-1, ::-1]
    coord = np.arange(SIDE)
    pick = np.arange(span)[:, None, None] == (SIDE - 1 - coord[:, None] + coord[None, :])[None]
    pick = jnp.asarray(pick.reshape(span, SIDE * SIDE), jnp.float32)
    table = jnp.einsum("hkj,jc->hkc", flipped, pick, precision=lax.Precision.HIGHEST)
    wide = jnp.transpose(table.reshape(heads, span, SIDE, SIDE), (0, 2, 1, 3))
    wide = wide.reshape(heads, SIDE, span * SIDE)
    return wide


def head_bias(wide_head):
    lanes = 128
    per = lanes // SIDE
    width = (SIDE - 1) // per * lanes + SIDE * SIDE
    shifted = [wide_head[:, SIDE * s : SIDE * s + width] for s in range(per)]
    rows = []
    for py in range(SIDE):
        start = (SIDE - 1 - py) * SIDE
        piece = shifted[start % lanes // SIDE]
        base = start // lanes * lanes
        rows.append(piece[:, base : base + SIDE * SIDE])
    return jnp.concatenate(rows, 0)


def project(rows, weight):
    return jnp.dot(rows, weight, preferred_element_type=jnp.float32).astype(jnp.bfloat16)


def body(
    latents,
    norm_gain,
    norm_bias,
    conv_weight,
    conv_bias,
    query_weight,
    key_weight,
    value_weight,
    out_weight,
    pos_table,
):
    frames, cells, width = latents.shape
    size = width // GROUPS
    devices = lax.axis_size("seq") * lax.axis_size("sub")
    place = place_of()
    own = latents[0]

    grouped = own.reshape(cells, GROUPS, size).astype(jnp.float32)
    partial = jnp.concatenate([jnp.sum(grouped, axis=(0, 2)), jnp.sum(grouped * grouped, axis=(0, 2))])
    got_a = lax.ppermute(own, AXES, [(0, 2)])
    got_b = lax.ppermute(own, AXES, [(1, 3)])
    start_a = jnp.where(place == 2, got_a, own)
    start_b = jnp.where(place == 3, got_b, own)
    stats, (start_a, start_b) = butterfly_sum(partial, devices, (start_a, start_b), 8)
    count = frames * devices * cells * size
    stats, pos_table, sent = lax.optimization_barrier((stats, pos_table, own))
    before = shifted(sent, devices, 1)
    before2 = shifted(sent, devices, 2)
    after = shifted(sent, devices, -1)
    wide = bias_table(pos_table)
    work = [(wide[h], head_bias) for h in range(wide.shape[0])]
    frame0, frame1, bias_all = broadcast_pair(start_a, start_b, place, devices, work, 4)
    mean = stats[:GROUPS] / count
    meansq = stats[GROUPS:] / count
    inv = lax.rsqrt(meansq - mean * mean + EPS)
    mean_c = jnp.repeat(mean, size)
    inv_c = jnp.repeat(inv, size)

    def norm(x):
        return ((x.astype(jnp.float32) - mean_c) * inv_c * norm_gain + norm_bias).astype(jnp.bfloat16)

    zero = jnp.zeros((cells, width), jnp.bfloat16)
    n_self = norm(own)
    n_before = jnp.where(place >= 1, norm(before), zero)
    n_before2 = jnp.where(place >= 2, norm(before2), zero)
    n_after = jnp.where(place + 1 < devices, norm(after), zero)
    n_0 = norm(frame0)
    n_1 = norm(frame1)

    taps = [
        jnp.concatenate([n_before2, n_before], 0),
        jnp.concatenate([n_before, n_self], 0),
        jnp.concatenate([n_self, n_after], 0),
    ]
    acc = jnp.zeros((2 * cells, width), jnp.float32)
    for tap in range(3):
        acc = acc + jnp.dot(taps[tap], conv_weight[tap], preferred_element_type=jnp.float32)
    mixed = (taps[1].astype(jnp.float32) + acc + conv_bias).astype(jnp.bfloat16)
    mixed_prev = mixed[:cells]
    mixed_self = mixed[cells:]
    acc0 = jnp.dot(n_0, conv_weight[1], preferred_element_type=jnp.float32)
    acc0 = acc0 + jnp.dot(n_1, conv_weight[2], preferred_element_type=jnp.float32)
    mixed_first = (n_0.astype(jnp.float32) + acc0 + conv_bias).astype(jnp.bfloat16)

    queries = project(mixed_self, query_weight)
    first_key = project(mixed_first, key_weight)
    first_value = project(mixed_first, value_weight)
    leading = place <= 1
    prev_key = jnp.where(leading, first_key, project(mixed_prev, key_weight))
    prev_value = jnp.where(leading, first_value, project(mixed_prev, value_weight))

    scale = HEAD_DIM ** (-0.5)
    per_head = []
    for head in range(width // HEAD_DIM):
        cols = slice(head * HEAD_DIM, (head + 1) * HEAD_DIM)
        bias_head = bias_all[head]
        key_block = jnp.concatenate([first_key[:, cols], prev_key[:, cols]], 0)
        value_block = jnp.concatenate([first_value[:, cols], prev_value[:, cols]], 0)
        scores = jnp.dot(queries[:, cols], key_block.T, preferred_element_type=jnp.float32) * scale
        scores = (scores.reshape(cells, 2, cells) + bias_head[:, None, :]).reshape(cells, 2 * cells)
        peak = jnp.max(scores, axis=1, keepdims=True)
        weights = jnp.exp(scores - peak)
        probs = (weights / jnp.sum(weights, axis=1, keepdims=True)).astype(jnp.bfloat16)
        per_head.append(jnp.dot(probs, value_block, preferred_element_type=jnp.float32).astype(jnp.bfloat16))
    attended = jnp.concatenate(per_head, 1)
    result = own.astype(jnp.float32) + jnp.dot(attended, out_weight, preferred_element_type=jnp.float32)
    return result.astype(jnp.bfloat16).reshape(frames, cells, width)


def solution(mesh):
    return jax.shard_map(
        body,
        mesh=mesh,
        in_specs=(P(AXES, None, None), P(), P(), P(), P(), P(), P(), P(), P(), P()),
        out_specs=P(AXES, None, None),
        check_vma=False,
    )
```

```python
import numpy as np
import jax
import jax.numpy as jnp
from jax import lax
from jax.sharding import PartitionSpec as P

SIDE = 32
HEAD_DIM = 64
GROUPS = 32

EPS = 1e-05
AXES = ("seq", "sub")


def place_of():
    return lax.axis_index("seq") * lax.axis_size("sub") + lax.axis_index("sub")


def shifted(array, devices, by):
    pairs = [(i, i + by) for i in range(devices) if 0 <= i + by < devices]
    return lax.ppermute(array, AXES, pairs)


def butterfly_sum(x, devices, tied, tie_at):
    step = 1
    while step < devices:
        if step == tie_at:
            x, tied = lax.optimization_barrier((x, tied))
        x = x + lax.ppermute(x, AXES, [(i, i ^ step) for i in range(devices)])
        step *= 2
    return x, tied


def broadcast_pair(first, second, place, devices, work, step=2, held=None):
    done = []
    rounds = 0
    while step < devices:
        got_a = lax.ppermute(first, AXES, [(i, i + step) for i in range(0, step, 2)])
        got_b = lax.ppermute(second, AXES, [(i, i + step) for i in range(1, step, 2)])
        fresh = (place >= step) & (place < 2 * step)
        first = jnp.where(fresh & (place % 2 == 0), got_a, first)
        second = jnp.where(fresh & (place % 2 == 1), got_b, second)
        if rounds < len(work) and work[rounds] is not None:
            if rounds == 0:
                first, second, operand, held = lax.optimization_barrier((first, second, work[rounds][0], held))
            else:
                first, second, operand = lax.optimization_barrier((first, second, work[rounds][0]))
            done.append(work[rounds][1](operand))
        rounds += 1
        step *= 2
    for item in work[rounds:]:
        done.append(item[1](item[0]))
    swap_a = lax.ppermute(first, AXES, [(i, i ^ 1) for i in range(devices)])
    swap_b = lax.ppermute(second, AXES, [(i, i ^ 1) for i in range(devices)])
    even = place % 2 == 0
    return jnp.where(even, first, swap_a), jnp.where(even, swap_b, second), done, held


def bias_table(pos_table):
    heads, span, _ = pos_table.shape
    flipped = pos_table[:, ::-1, ::-1]
    coord = np.arange(SIDE)
    pick = np.arange(span)[:, None, None] == (SIDE - 1 - coord[:, None] + coord[None, :])[None]
    pick = jnp.asarray(pick.reshape(span, SIDE * SIDE), jnp.float32)
    table = jnp.einsum("hkj,jc->hkc", flipped, pick, precision=lax.Precision.HIGHEST)
    wide = jnp.transpose(table.reshape(heads, span, SIDE, SIDE), (0, 2, 1, 3))
    wide = wide.reshape(heads, SIDE, span * SIDE)
    return wide


def head_bias(wide_head):
    lanes = 128
    per = lanes // SIDE
    width = (SIDE - 1) // per * lanes + SIDE * SIDE
    shifted = [wide_head[:, SIDE * s : SIDE * s + width] for s in range(per)]
    rows = []
    for py in range(SIDE):
        start = (SIDE - 1 - py) * SIDE
        piece = shifted[start % lanes // SIDE]
        base = start // lanes * lanes
        rows.append(piece[:, base : base + SIDE * SIDE])
    return jnp.concatenate(rows, 0)


def project(rows, weight):
    return jnp.dot(rows, weight, preferred_element_type=jnp.float32).astype(jnp.bfloat16)


def body(
    latents,
    norm_gain,
    norm_bias,
    conv_weight,
    conv_bias,
    query_weight,
    key_weight,
    value_weight,
    out_weight,
    pos_table,
):
    frames, cells, width = latents.shape
    size = width // GROUPS
    devices = lax.axis_size("seq") * lax.axis_size("sub")
    place = place_of()
    own = latents[0]

    grouped = own.reshape(cells, GROUPS, size).astype(jnp.float32)
    partial = jnp.concatenate([jnp.sum(grouped, axis=(0, 2)), jnp.sum(grouped * grouped, axis=(0, 2))])
    got_a = lax.ppermute(own, AXES, [(0, 2)])
    got_b = lax.ppermute(own, AXES, [(1, 3)])
    start_a = jnp.where(place == 2, got_a, own)
    start_b = jnp.where(place == 3, got_b, own)
    stats, (start_a, start_b) = butterfly_sum(partial, devices, (start_a, start_b), 8)
    count = frames * devices * cells * size
    stats, pos_table = lax.optimization_barrier((stats, pos_table))
    wide = bias_table(pos_table)
    work = [(wide[h], head_bias) for h in range(wide.shape[0])]
    frame0, frame1, bias_all, sent = broadcast_pair(start_a, start_b, place, devices, work, 4, own)
    before = shifted(sent, devices, 1)
    before2 = shifted(sent, devices, 2)
    after = shifted(sent, devices, -1)
    mean = stats[:GROUPS] / count
    meansq = stats[GROUPS:] / count
    inv = lax.rsqrt(meansq - mean * mean + EPS)
    mean_c = jnp.repeat(mean, size)
    inv_c = jnp.repeat(inv, size)

    def norm(x):
        return ((x.astype(jnp.float32) - mean_c) * inv_c * norm_gain + norm_bias).astype(jnp.bfloat16)

    zero = jnp.zeros((cells, width), jnp.bfloat16)
    n_self = norm(own)
    n_before = jnp.where(place >= 1, norm(before), zero)
    n_before2 = jnp.where(place >= 2, norm(before2), zero)
    n_after = jnp.where(place + 1 < devices, norm(after), zero)
    n_0 = norm(frame0)
    n_1 = norm(frame1)

    taps = [
        jnp.concatenate([n_before2, n_before], 0),
        jnp.concatenate([n_before, n_self], 0),
        jnp.concatenate([n_self, n_after], 0),
    ]
    acc = jnp.zeros((2 * cells, width), jnp.float32)
    for tap in range(3):
        acc = acc + jnp.dot(taps[tap], conv_weight[tap], preferred_element_type=jnp.float32)
    mixed = (taps[1].astype(jnp.float32) + acc + conv_bias).astype(jnp.bfloat16)
    mixed_prev = mixed[:cells]
    mixed_self = mixed[cells:]
    acc0 = jnp.dot(n_0, conv_weight[1], preferred_element_type=jnp.float32)
    acc0 = acc0 + jnp.dot(n_1, conv_weight[2], preferred_element_type=jnp.float32)
    mixed_first = (n_0.astype(jnp.float32) + acc0 + conv_bias).astype(jnp.bfloat16)

    queries = project(mixed_self, query_weight)
    first_key = project(mixed_first, key_weight)
    first_value = project(mixed_first, value_weight)
    leading = place <= 1
    prev_key = jnp.where(leading, first_key, project(mixed_prev, key_weight))
    prev_value = jnp.where(leading, first_value, project(mixed_prev, value_weight))

    scale = HEAD_DIM ** (-0.5)
    per_head = []
    for head in range(width // HEAD_DIM):
        cols = slice(head * HEAD_DIM, (head + 1) * HEAD_DIM)
        bias_head = bias_all[head]
        key_block = jnp.concatenate([first_key[:, cols], prev_key[:, cols]], 0)
        value_block = jnp.concatenate([first_value[:, cols], prev_value[:, cols]], 0)
        scores = jnp.dot(queries[:, cols], key_block.T, preferred_element_type=jnp.float32) * scale
        scores = (scores.reshape(cells, 2, cells) + bias_head[:, None, :]).reshape(cells, 2 * cells)
        peak = jnp.max(scores, axis=1, keepdims=True)
        weights = jnp.exp(scores - peak)
        probs = (weights / jnp.sum(weights, axis=1, keepdims=True)).astype(jnp.bfloat16)
        per_head.append(jnp.dot(probs, value_block, preferred_element_type=jnp.float32).astype(jnp.bfloat16))
    attended = jnp.concatenate(per_head, 1)
    result = own.astype(jnp.float32) + jnp.dot(attended, out_weight, preferred_element_type=jnp.float32)
    return result.astype(jnp.bfloat16).reshape(frames, cells, width)


def solution(mesh):
    return jax.shard_map(
        body,
        mesh=mesh,
        in_specs=(P(AXES, None, None), P(), P(), P(), P(), P(), P(), P(), P(), P()),
        out_specs=P(AXES, None, None),
        check_vma=False,
    )
```

```python
import numpy as np
import jax
import jax.numpy as jnp
from jax import lax
from jax.sharding import PartitionSpec as P

SIDE = 32
HEAD_DIM = 64
GROUPS = 32

EPS = 1e-05
AXES = ("seq", "sub")


def place_of():
    return lax.axis_index("seq") * lax.axis_size("sub") + lax.axis_index("sub")


def shifted(array, devices, by):
    pairs = [(i, i + by) for i in range(devices) if 0 <= i + by < devices]
    return lax.ppermute(array, AXES, pairs)


def butterfly_sum(x, devices, ties):
    step = 1
    made = None
    while step < devices:
        if step in ties:
            x, made = lax.optimization_barrier((x, ties[step](made)))
        x = x + lax.ppermute(x, AXES, [(i, i ^ step) for i in range(devices)])
        step *= 2
    return x, made


def broadcast_pair(first, second, place, devices, work, step=2):
    done = []
    rounds = 0
    while step < devices:
        got_a = lax.ppermute(first, AXES, [(i, i + step) for i in range(0, step, 2)])
        got_b = lax.ppermute(second, AXES, [(i, i + step) for i in range(1, step, 2)])
        fresh = (place >= step) & (place < 2 * step)
        first = jnp.where(fresh & (place % 2 == 0), got_a, first)
        second = jnp.where(fresh & (place % 2 == 1), got_b, second)
        if rounds < len(work) and work[rounds] is not None:
            first, second, operand = lax.optimization_barrier((first, second, work[rounds][0]))
            done.append(work[rounds][1](operand))
        rounds += 1
        step *= 2
    for item in work[rounds:]:
        done.append(item[1](item[0]))
    swap_a = lax.ppermute(first, AXES, [(i, i ^ 1) for i in range(devices)])
    swap_b = lax.ppermute(second, AXES, [(i, i ^ 1) for i in range(devices)])
    even = place % 2 == 0
    return jnp.where(even, first, swap_a), jnp.where(even, swap_b, second), done


def bias_table(pos_table):
    heads, span, _ = pos_table.shape
    flipped = pos_table[:, ::-1, ::-1]
    coord = np.arange(SIDE)
    pick = np.arange(span)[:, None, None] == (SIDE - 1 - coord[:, None] + coord[None, :])[None]
    pick = jnp.asarray(pick.reshape(span, SIDE * SIDE), jnp.float32)
    table = jnp.einsum("hkj,jc->hkc", flipped, pick, precision=lax.Precision.HIGHEST)
    wide = jnp.transpose(table.reshape(heads, span, SIDE, SIDE), (0, 2, 1, 3))
    wide = wide.reshape(heads, SIDE, span * SIDE)
    return wide


def head_bias(wide_head):
    lanes = 128
    per = lanes // SIDE
    width = (SIDE - 1) // per * lanes + SIDE * SIDE
    shifted = [wide_head[:, SIDE * s : SIDE * s + width] for s in range(per)]
    rows = []
    for py in range(SIDE):
        start = (SIDE - 1 - py) * SIDE
        piece = shifted[start % lanes // SIDE]
        base = start // lanes * lanes
        rows.append(piece[:, base : base + SIDE * SIDE])
    return jnp.concatenate(rows, 0)


def project(rows, weight):
    return jnp.dot(rows, weight, preferred_element_type=jnp.float32).astype(jnp.bfloat16)


def body(
    latents,
    norm_gain,
    norm_bias,
    conv_weight,
    conv_bias,
    query_weight,
    key_weight,
    value_weight,
    out_weight,
    pos_table,
):
    frames, cells, width = latents.shape
    size = width // GROUPS
    devices = lax.axis_size("seq") * lax.axis_size("sub")
    place = place_of()
    own = latents[0]

    grouped = own.reshape(cells, GROUPS, size).astype(jnp.float32)
    partial = jnp.concatenate([jnp.sum(grouped, axis=(0, 2)), jnp.sum(grouped * grouped, axis=(0, 2))])
    def tree_round(held, step):
        first, second = (own, own) if held is None else held
        got_a = lax.ppermute(first, AXES, [(i, i + step) for i in range(0, step, 2)])
        got_b = lax.ppermute(second, AXES, [(i, i + step) for i in range(1, step, 2)])
        fresh = (place >= step) & (place < 2 * step)
        return (jnp.where(fresh & (place % 2 == 0), got_a, first),
                jnp.where(fresh & (place % 2 == 1), got_b, second))

    ties = {4: lambda held: tree_round(held, 2), 32: lambda held: tree_round(held, 4)}
    stats, (start_a, start_b) = butterfly_sum(partial, devices, ties)
    count = frames * devices * cells * size
    stats, pos_table, sent = lax.optimization_barrier((stats, pos_table, own))
    before = shifted(sent, devices, 1)
    before2 = shifted(sent, devices, 2)
    after = shifted(sent, devices, -1)
    wide = bias_table(pos_table)
    work = [(wide[h], head_bias) for h in range(wide.shape[0])]
    frame0, frame1, bias_all = broadcast_pair(start_a, start_b, place, devices, work, 8)
    mean = stats[:GROUPS] / count
    meansq = stats[GROUPS:] / count
    inv = lax.rsqrt(meansq - mean * mean + EPS)
    mean_c = jnp.repeat(mean, size)
    inv_c = jnp.repeat(inv, size)

    def norm(x):
        return ((x.astype(jnp.float32) - mean_c) * inv_c * norm_gain + norm_bias).astype(jnp.bfloat16)

    zero = jnp.zeros((cells, width), jnp.bfloat16)
    n_self = norm(own)
    n_before = jnp.where(place >= 1, norm(before), zero)
    n_before2 = jnp.where(place >= 2, norm(before2), zero)
    n_after = jnp.where(place + 1 < devices, norm(after), zero)
    n_0 = norm(frame0)
    n_1 = norm(frame1)

    taps = [
        jnp.concatenate([n_before2, n_before], 0),
        jnp.concatenate([n_before, n_self], 0),
        jnp.concatenate([n_self, n_after], 0),
    ]
    acc = jnp.zeros((2 * cells, width), jnp.float32)
    for tap in range(3):
        acc = acc + jnp.dot(taps[tap], conv_weight[tap], preferred_element_type=jnp.float32)
    mixed = (taps[1].astype(jnp.float32) + acc + conv_bias).astype(jnp.bfloat16)
    mixed_prev = mixed[:cells]
    mixed_self = mixed[cells:]
    acc0 = jnp.dot(n_0, conv_weight[1], preferred_element_type=jnp.float32)
    acc0 = acc0 + jnp.dot(n_1, conv_weight[2], preferred_element_type=jnp.float32)
    mixed_first = (n_0.astype(jnp.float32) + acc0 + conv_bias).astype(jnp.bfloat16)

    queries = project(mixed_self, query_weight)
    first_key = project(mixed_first, key_weight)
    first_value = project(mixed_first, value_weight)
    leading = place <= 1
    prev_key = jnp.where(leading, first_key, project(mixed_prev, key_weight))
    prev_value = jnp.where(leading, first_value, project(mixed_prev, value_weight))

    scale = HEAD_DIM ** (-0.5)
    per_head = []
    for head in range(width // HEAD_DIM):
        cols = slice(head * HEAD_DIM, (head + 1) * HEAD_DIM)
        bias_head = bias_all[head]
        key_block = jnp.concatenate([first_key[:, cols], prev_key[:, cols]], 0)
        value_block = jnp.concatenate([first_value[:, cols], prev_value[:, cols]], 0)
        scores = jnp.dot(queries[:, cols], key_block.T, preferred_element_type=jnp.float32) * scale
        scores = (scores.reshape(cells, 2, cells) + bias_head[:, None, :]).reshape(cells, 2 * cells)
        peak = jnp.max(scores, axis=1, keepdims=True)
        weights = jnp.exp(scores - peak)
        probs = (weights / jnp.sum(weights, axis=1, keepdims=True)).astype(jnp.bfloat16)
        per_head.append(jnp.dot(probs, value_block, preferred_element_type=jnp.float32).astype(jnp.bfloat16))
    attended = jnp.concatenate(per_head, 1)
    result = own.astype(jnp.float32) + jnp.dot(attended, out_weight, preferred_element_type=jnp.float32)
    return result.astype(jnp.bfloat16).reshape(frames, cells, width)


def solution(mesh):
    return jax.shard_map(
        body,
        mesh=mesh,
        in_specs=(P(AXES, None, None), P(), P(), P(), P(), P(), P(), P(), P(), P()),
        out_specs=P(AXES, None, None),
        check_vma=False,
    )
```

```python
import numpy as np
import jax
import jax.numpy as jnp
from jax import lax
from jax.sharding import PartitionSpec as P

SIDE = 32
HEAD_DIM = 64
GROUPS = 32

EPS = 1e-05
AXES = ("seq", "sub")


def place_of():
    return lax.axis_index("seq") * lax.axis_size("sub") + lax.axis_index("sub")


def shifted(array, devices, by):
    pairs = [(i, i + by) for i in range(devices) if 0 <= i + by < devices]
    return lax.ppermute(array, AXES, pairs)


def butterfly_sum(x, devices, tied, tie_at):
    step = 1
    while step < devices:
        if step == tie_at:
            x, tied = lax.optimization_barrier((x, tied))
        x = x + lax.ppermute(x, AXES, [(i, i ^ step) for i in range(devices)])
        step *= 2
    return x, tied


def broadcast_pair(first, second, place, devices, work, step=2):
    done = []
    rounds = 0
    while step < devices:
        got_a = lax.ppermute(first, AXES, [(i, i + step) for i in range(0, step, 2)])
        got_b = lax.ppermute(second, AXES, [(i, i + step) for i in range(1, step, 2)])
        fresh = (place >= step) & (place < 2 * step)
        first = jnp.where(fresh & (place % 2 == 0), got_a, first)
        second = jnp.where(fresh & (place % 2 == 1), got_b, second)
        if rounds < len(work) and work[rounds] is not None:
            first, second, operand = lax.optimization_barrier((first, second, work[rounds][0]))
            done.append(work[rounds][1](operand))
        rounds += 1
        step *= 2
    for item in work[rounds:]:
        done.append(item[1](item[0]))
    swap_a = lax.ppermute(first, AXES, [(i, i ^ 1) for i in range(devices)])
    swap_b = lax.ppermute(second, AXES, [(i, i ^ 1) for i in range(devices)])
    even = place % 2 == 0
    return jnp.where(even, first, swap_a), jnp.where(even, swap_b, second), done


def bias_table(pos_table):
    heads, span, _ = pos_table.shape
    flipped = pos_table[:, ::-1, ::-1]
    coord = np.arange(SIDE)
    pick = np.arange(span)[:, None, None] == (SIDE - 1 - coord[:, None] + coord[None, :])[None]
    pick = jnp.asarray(pick.reshape(span, SIDE * SIDE), jnp.float32)
    table = jnp.einsum("hkj,jc->hkc", flipped, pick, precision=lax.Precision.HIGHEST)
    wide = jnp.transpose(table.reshape(heads, span, SIDE, SIDE), (0, 2, 1, 3))
    wide = wide.reshape(heads, SIDE, span * SIDE)
    return wide


def head_bias(wide_head):
    lanes = 128
    per = lanes // SIDE
    width = (SIDE - 1) // per * lanes + SIDE * SIDE
    shifted = [wide_head[:, SIDE * s : SIDE * s + width] for s in range(per)]
    rows = []
    for py in range(SIDE):
        start = (SIDE - 1 - py) * SIDE
        piece = shifted[start % lanes // SIDE]
        base = start // lanes * lanes
        rows.append(piece[:, base : base + SIDE * SIDE])
    return jnp.concatenate(rows, 0)


def project(rows, weight):
    return jnp.dot(rows, weight, preferred_element_type=jnp.float32).astype(jnp.bfloat16)


def body(
    latents,
    norm_gain,
    norm_bias,
    conv_weight,
    conv_bias,
    query_weight,
    key_weight,
    value_weight,
    out_weight,
    pos_table,
):
    frames, cells, width = latents.shape
    size = width // GROUPS
    devices = lax.axis_size("seq") * lax.axis_size("sub")
    place = place_of()
    own = latents[0]

    grouped = own.reshape(cells, GROUPS, size).astype(jnp.float32)
    partial = jnp.concatenate([jnp.sum(grouped, axis=(0, 2)), jnp.sum(grouped * grouped, axis=(0, 2))])
    got_a = lax.ppermute(own, AXES, [(0, 2)])
    got_b = lax.ppermute(own, AXES, [(1, 3)])
    start_a = jnp.where(place == 2, got_a, own)
    start_b = jnp.where(place == 3, got_b, own)
    stats, (start_a, start_b) = butterfly_sum(partial, devices, (start_a, start_b), 8)
    count = frames * devices * cells * size
    stats, pos_table, sent = lax.optimization_barrier((stats, pos_table, own))
    before = shifted(sent, devices, 1)
    before2 = shifted(sent, devices, 2)
    after = shifted(sent, devices, -1)
    wide = bias_table(pos_table)
    work = [(wide[h], head_bias) for h in range(wide.shape[0])]
    frame0, frame1, bias_all = broadcast_pair(start_a, start_b, place, devices, work, 4)
    mean = stats[:GROUPS] / count
    meansq = stats[GROUPS:] / count
    inv = lax.rsqrt(meansq - mean * mean + EPS)
    mean_c = jnp.repeat(mean, size)
    inv_c = jnp.repeat(inv, size)

    def norm(x):
        return ((x.astype(jnp.float32) - mean_c) * inv_c * norm_gain + norm_bias).astype(jnp.bfloat16)

    zero = jnp.zeros((cells, width), jnp.bfloat16)
    n_self = norm(own)
    n_before = jnp.where(place >= 1, norm(before), zero)
    n_before2 = jnp.where(place >= 2, norm(before2), zero)
    n_after = jnp.where(place + 1 < devices, norm(after), zero)
    n_0 = norm(frame0)
    n_1 = norm(frame1)

    taps = [
        jnp.concatenate([n_before2, n_before], 0),
        jnp.concatenate([n_before, n_self], 0),
        jnp.concatenate([n_self, n_after], 0),
    ]
    acc = jnp.zeros((2 * cells, width), jnp.float32)
    for tap in range(3):
        acc = acc + jnp.dot(taps[tap], conv_weight[tap], preferred_element_type=jnp.float32)
    mixed = (taps[1].astype(jnp.float32) + acc + conv_bias).astype(jnp.bfloat16)
    mixed_prev = mixed[:cells]
    mixed_self = mixed[cells:]
    acc0 = jnp.dot(n_0, conv_weight[1], preferred_element_type=jnp.float32)
    acc0 = acc0 + jnp.dot(n_1, conv_weight[2], preferred_element_type=jnp.float32)
    mixed_first = (n_0.astype(jnp.float32) + acc0 + conv_bias).astype(jnp.bfloat16)

    queries = project(mixed_self, query_weight)
    first_key = project(mixed_first, key_weight)
    first_value = project(mixed_first, value_weight)
    leading = place <= 1
    prev_key = jnp.where(leading, first_key, project(mixed_prev, key_weight))
    prev_value = jnp.where(leading, first_value, project(mixed_prev, value_weight))

    scale = HEAD_DIM ** (-0.5)
    per_head = []
    for head in range(width // HEAD_DIM):
        cols = slice(head * HEAD_DIM, (head + 1) * HEAD_DIM)
        bias_head = bias_all[head]
        key_block = jnp.concatenate([first_key[:, cols], prev_key[:, cols]], 0)
        value_block = jnp.concatenate([first_value[:, cols], prev_value[:, cols]], 0)
        scores = jnp.dot(queries[:, cols], key_block.T, preferred_element_type=jnp.float32) * scale
        scores = (scores.reshape(cells, 2, cells) + bias_head[:, None, :]).reshape(cells, 2 * cells)
        peak = jnp.max(scores, axis=1, keepdims=True)
        weights = jnp.exp(scores - peak)
        probs = (weights * (1.0 / jnp.sum(weights, axis=1, keepdims=True))).astype(jnp.bfloat16)
        per_head.append(jnp.dot(probs, value_block, preferred_element_type=jnp.float32).astype(jnp.bfloat16))
    attended = jnp.concatenate(per_head, 1)
    result = own.astype(jnp.float32) + jnp.dot(attended, out_weight, preferred_element_type=jnp.float32)
    return result.astype(jnp.bfloat16).reshape(frames, cells, width)


def solution(mesh):
    return jax.shard_map(
        body,
        mesh=mesh,
        in_specs=(P(AXES, None, None), P(), P(), P(), P(), P(), P(), P(), P(), P()),
        out_specs=P(AXES, None, None),
        check_vma=False,
    )
```

```python
import numpy as np
import jax
import jax.numpy as jnp
from jax import lax
from jax.sharding import PartitionSpec as P

SIDE = 32
HEAD_DIM = 64
GROUPS = 32

EPS = 1e-05
AXES = ("seq", "sub")


def place_of():
    return lax.axis_index("seq") * lax.axis_size("sub") + lax.axis_index("sub")


def shifted(array, devices, by):
    pairs = [(i, i + by) for i in range(devices) if 0 <= i + by < devices]
    return lax.ppermute(array, AXES, pairs)


def butterfly_sum(x, devices, tied, tie_at):
    step = 1
    while step < devices:
        if step == tie_at:
            x, tied = lax.optimization_barrier((x, tied))
        x = x + lax.ppermute(x, AXES, [(i, i ^ step) for i in range(devices)])
        step *= 2
    return x, tied


def broadcast_pair(first, second, place, devices, work, step=2):
    done = []
    rounds = 0
    while step < devices:
        got_a = lax.ppermute(first, AXES, [(i, i + step) for i in range(0, step, 2)])
        got_b = lax.ppermute(second, AXES, [(i, i + step) for i in range(1, step, 2)])
        fresh = (place >= step) & (place < 2 * step)
        first = jnp.where(fresh & (place % 2 == 0), got_a, first)
        second = jnp.where(fresh & (place % 2 == 1), got_b, second)
        if rounds < len(work) and work[rounds] is not None:
            first, second, operand = lax.optimization_barrier((first, second, work[rounds][0]))
            done.append(work[rounds][1](operand))
        rounds += 1
        step *= 2
    for item in work[rounds:]:
        done.append(item[1](item[0]))
    swap_a = lax.ppermute(first, AXES, [(i, i ^ 1) for i in range(devices)])
    swap_b = lax.ppermute(second, AXES, [(i, i ^ 1) for i in range(devices)])
    even = place % 2 == 0
    return jnp.where(even, first, swap_a), jnp.where(even, swap_b, second), done


def bias_table(pos_table):
    heads, span, _ = pos_table.shape
    flipped = pos_table[:, ::-1, ::-1]
    coord = np.arange(SIDE)
    pick = np.arange(span)[:, None, None] == (SIDE - 1 - coord[:, None] + coord[None, :])[None]
    pick = jnp.asarray(pick.reshape(span, SIDE * SIDE), jnp.float32)
    table = jnp.einsum("hkj,jc->hkc", flipped, pick, precision=lax.Precision.HIGHEST)
    wide = jnp.transpose(table.reshape(heads, span, SIDE, SIDE), (0, 2, 1, 3))
    wide = wide.reshape(heads, SIDE, span * SIDE)
    return wide


def head_bias(wide_head):
    lanes = 128
    per = lanes // SIDE
    width = (SIDE - 1) // per * lanes + SIDE * SIDE
    shifted = [wide_head[:, SIDE * s : SIDE * s + width] for s in range(per)]
    rows = []
    for py in range(SIDE):
        start = (SIDE - 1 - py) * SIDE
        piece = shifted[start % lanes // SIDE]
        base = start // lanes * lanes
        rows.append(piece[:, base : base + SIDE * SIDE])
    return jnp.concatenate(rows, 0)


def project(rows, weight):
    return jnp.dot(rows, weight, preferred_element_type=jnp.float32).astype(jnp.bfloat16)


def body(
    latents,
    norm_gain,
    norm_bias,
    conv_weight,
    conv_bias,
    query_weight,
    key_weight,
    value_weight,
    out_weight,
    pos_table,
):
    frames, cells, width = latents.shape
    size = width // GROUPS
    devices = lax.axis_size("seq") * lax.axis_size("sub")
    place = place_of()
    own = latents[0]

    grouped = own.reshape(cells, GROUPS, size).astype(jnp.float32)
    partial = jnp.concatenate([jnp.sum(grouped, axis=(0, 2)), jnp.sum(grouped * grouped, axis=(0, 2))])
    got_a = lax.ppermute(own, AXES, [(0, 2)])
    got_b = lax.ppermute(own, AXES, [(1, 3)])
    start_a = jnp.where(place == 2, got_a, own)
    start_b = jnp.where(place == 3, got_b, own)
    stats, (start_a, start_b) = butterfly_sum(partial, devices, (start_a, start_b), 8)
    count = frames * devices * cells * size
    stats, pos_table, sent = lax.optimization_barrier((stats, pos_table, own))
    before = shifted(sent, devices, 1)
    before2 = shifted(sent, devices, 2)
    after = shifted(sent, devices, -1)
    wide = bias_table(pos_table)
    work = [(wide[h], head_bias) for h in range(wide.shape[0])]
    frame0, frame1, bias_all = broadcast_pair(start_a, start_b, place, devices, work, 4)
    mean = stats[:GROUPS] / count
    meansq = stats[GROUPS:] / count
    inv = lax.rsqrt(meansq - mean * mean + EPS)
    mean_c = jnp.repeat(mean, size)
    inv_c = jnp.repeat(inv, size)

    def norm(x):
        return ((x.astype(jnp.float32) - mean_c) * inv_c * norm_gain + norm_bias).astype(jnp.bfloat16)

    zero = jnp.zeros((cells, width), jnp.bfloat16)
    n_self = norm(own)
    n_before = jnp.where(place >= 1, norm(before), zero)
    n_before2 = jnp.where(place >= 2, norm(before2), zero)
    n_after = jnp.where(place + 1 < devices, norm(after), zero)
    n_0 = norm(frame0)
    n_1 = norm(frame1)

    taps = [
        jnp.concatenate([n_before2, n_before], 0),
        jnp.concatenate([n_before, n_self], 0),
        jnp.concatenate([n_self, n_after], 0),
    ]
    acc = jnp.zeros((2 * cells, width), jnp.float32)
    for tap in range(3):
        acc = acc + jnp.dot(taps[tap], conv_weight[tap], preferred_element_type=jnp.float32)
    mixed = (taps[1].astype(jnp.float32) + acc + conv_bias).astype(jnp.bfloat16)
    mixed_prev = mixed[:cells]
    mixed_self = mixed[cells:]
    acc0 = jnp.dot(n_0, conv_weight[1], preferred_element_type=jnp.float32)
    acc0 = acc0 + jnp.dot(n_1, conv_weight[2], preferred_element_type=jnp.float32)
    mixed_first = (n_0.astype(jnp.float32) + acc0 + conv_bias).astype(jnp.bfloat16)

    queries = project(mixed_self, query_weight)
    first_key = project(mixed_first, key_weight)
    first_value = project(mixed_first, value_weight)
    leading = place <= 1
    prev_key = jnp.where(leading, first_key, project(mixed_prev, key_weight))
    prev_value = jnp.where(leading, first_value, project(mixed_prev, value_weight))

    scale = HEAD_DIM ** (-0.5)
    per_head = []
    chunk = cells // 2
    for head in range(width // HEAD_DIM):
        cols = slice(head * HEAD_DIM, (head + 1) * HEAD_DIM)
        key_block = jnp.concatenate([first_key[:, cols], prev_key[:, cols]], 0)
        value_block = jnp.concatenate([first_value[:, cols], prev_value[:, cols]], 0)
        parts = []
        for row in range(0, cells, chunk):
            bias_rows = bias_all[head][row : row + chunk]
            scores = (
                jnp.dot(queries[row : row + chunk, cols], key_block.T, preferred_element_type=jnp.float32)
                * scale
            )
            scores = (scores.reshape(chunk, 2, cells) + bias_rows[:, None, :]).reshape(chunk, 2 * cells)
            peak = jnp.max(scores, axis=1, keepdims=True)
            weights = jnp.exp(scores - peak)
            probs = (weights / jnp.sum(weights, axis=1, keepdims=True)).astype(jnp.bfloat16)
            parts.append(jnp.dot(probs, value_block, preferred_element_type=jnp.float32).astype(jnp.bfloat16))
        per_head.append(jnp.concatenate(parts, 0))
    attended = jnp.concatenate(per_head, 1)
    result = own.astype(jnp.float32) + jnp.dot(attended, out_weight, preferred_element_type=jnp.float32)
    return result.astype(jnp.bfloat16).reshape(frames, cells, width)


def solution(mesh):
    return jax.shard_map(
        body,
        mesh=mesh,
        in_specs=(P(AXES, None, None), P(), P(), P(), P(), P(), P(), P(), P(), P()),
        out_specs=P(AXES, None, None),
        check_vma=False,
    )
```

```python
import numpy as np
import jax
import jax.numpy as jnp
from jax import lax
from jax.sharding import PartitionSpec as P

SIDE = 32
HEAD_DIM = 64
GROUPS = 32

EPS = 1e-05
AXES = ("seq", "sub")


def place_of():
    return lax.axis_index("seq") * lax.axis_size("sub") + lax.axis_index("sub")


def shifted(array, devices, by):
    pairs = [(i, i + by) for i in range(devices) if 0 <= i + by < devices]
    return lax.ppermute(array, AXES, pairs)


def butterfly_sum(x, devices, tied, tie_at):
    step = 1
    while step < devices:
        if step == tie_at:
            x, tied = lax.optimization_barrier((x, tied))
        x = x + lax.ppermute(x, AXES, [(i, i ^ step) for i in range(devices)])
        step *= 2
    return x, tied


def broadcast_pair(first, second, place, devices, work, step=2):
    done = []
    rounds = 0
    while step < devices:
        got_a = lax.ppermute(first, AXES, [(i, i + step) for i in range(0, step, 2)])
        got_b = lax.ppermute(second, AXES, [(i, i + step) for i in range(1, step, 2)])
        fresh = (place >= step) & (place < 2 * step)
        first = jnp.where(fresh & (place % 2 == 0), got_a, first)
        second = jnp.where(fresh & (place % 2 == 1), got_b, second)
        if rounds < len(work) and work[rounds] is not None:
            first, second, operand = lax.optimization_barrier((first, second, work[rounds][0]))
            done.append(work[rounds][1](operand))
        rounds += 1
        step *= 2
    for item in work[rounds:]:
        done.append(item[1](item[0]))
    swap_a = lax.ppermute(first, AXES, [(i, i ^ 1) for i in range(devices)])
    swap_b = lax.ppermute(second, AXES, [(i, i ^ 1) for i in range(devices)])
    even = place % 2 == 0
    return jnp.where(even, first, swap_a), jnp.where(even, swap_b, second), done


def bias_table(pos_table):
    heads, span, _ = pos_table.shape
    flipped = pos_table[:, ::-1, ::-1]
    coord = np.arange(SIDE)
    pick = np.arange(span)[:, None, None] == (SIDE - 1 - coord[:, None] + coord[None, :])[None]
    pick = jnp.asarray(pick.reshape(span, SIDE * SIDE), jnp.float32)
    table = jnp.einsum("hkj,jc->hkc", flipped, pick, precision=lax.Precision.HIGHEST)
    wide = jnp.transpose(table.reshape(heads, span, SIDE, SIDE), (0, 2, 1, 3))
    wide = wide.reshape(heads, SIDE, span * SIDE)
    return wide


def head_bias(wide_head):
    lanes = 128
    per = lanes // SIDE
    width = (SIDE - 1) // per * lanes + SIDE * SIDE
    shifted = [wide_head[:, SIDE * s : SIDE * s + width] for s in range(per)]
    rows = []
    for py in range(SIDE):
        start = (SIDE - 1 - py) * SIDE
        piece = shifted[start % lanes // SIDE]
        base = start // lanes * lanes
        rows.append(piece[:, base : base + SIDE * SIDE])
    return jnp.concatenate(rows, 0)


def project(rows, weight):
    return jnp.dot(rows, weight, preferred_element_type=jnp.float32).astype(jnp.bfloat16)


def body(
    latents,
    norm_gain,
    norm_bias,
    conv_weight,
    conv_bias,
    query_weight,
    key_weight,
    value_weight,
    out_weight,
    pos_table,
):
    frames, cells, width = latents.shape
    size = width // GROUPS
    devices = lax.axis_size("seq") * lax.axis_size("sub")
    place = place_of()
    own = latents[0]

    grouped = own.reshape(cells, GROUPS, size).astype(jnp.float32)
    partial = jnp.concatenate([jnp.sum(grouped, axis=(0, 2)), jnp.sum(grouped * grouped, axis=(0, 2))])
    got_a = lax.ppermute(own, AXES, [(0, 2)])
    got_b = lax.ppermute(own, AXES, [(1, 3)])
    start_a = jnp.where(place == 2, got_a, own)
    start_b = jnp.where(place == 3, got_b, own)
    stats, (start_a, start_b) = butterfly_sum(partial, devices, (start_a, start_b), 8)
    count = frames * devices * cells * size
    stats, pos_table, sent = lax.optimization_barrier((stats, pos_table, own))
    before = shifted(sent, devices, 1)
    before2 = shifted(sent, devices, 2)
    after = shifted(sent, devices, -1)
    wide = bias_table(pos_table)
    work = [(wide[h], head_bias) for h in range(wide.shape[0])]
    frame0, frame1, bias_all = broadcast_pair(start_a, start_b, place, devices, work, 4)
    mean = stats[:GROUPS] / count
    meansq = stats[GROUPS:] / count
    inv = lax.rsqrt(meansq - mean * mean + EPS)
    mean_c = jnp.repeat(mean, size)
    inv_c = jnp.repeat(inv, size)

    def norm(x):
        return ((x.astype(jnp.float32) - mean_c) * inv_c * norm_gain + norm_bias).astype(jnp.bfloat16)

    zero = jnp.zeros((cells, width), jnp.bfloat16)
    n_self = norm(own)
    n_before = jnp.where(place >= 1, norm(before), zero)
    n_before2 = jnp.where(place >= 2, norm(before2), zero)
    n_after = jnp.where(place + 1 < devices, norm(after), zero)
    n_0 = norm(frame0)
    n_1 = norm(frame1)

    taps = [
        jnp.concatenate([n_before2, n_before], 0),
        jnp.concatenate([n_before, n_self], 0),
        jnp.concatenate([n_self, n_after], 0),
    ]
    acc = jnp.zeros((2 * cells, width), jnp.float32)
    for tap in range(3):
        acc = acc + jnp.dot(taps[tap], conv_weight[tap], preferred_element_type=jnp.float32)
    mixed = (taps[1].astype(jnp.float32) + acc + conv_bias).astype(jnp.bfloat16)
    mixed_prev = mixed[:cells]
    mixed_self = mixed[cells:]
    acc0 = jnp.dot(n_0, conv_weight[1], preferred_element_type=jnp.float32)
    acc0 = acc0 + jnp.dot(n_1, conv_weight[2], preferred_element_type=jnp.float32)
    mixed_first = (n_0.astype(jnp.float32) + acc0 + conv_bias).astype(jnp.bfloat16)

    queries = project(mixed_self, query_weight)
    first_key = project(mixed_first, key_weight)
    first_value = project(mixed_first, value_weight)
    leading = place <= 1
    prev_key = jnp.where(leading, first_key, project(mixed_prev, key_weight))
    prev_value = jnp.where(leading, first_value, project(mixed_prev, value_weight))

    scale = HEAD_DIM ** (-0.5)
    per_head = []
    for head in range(width // HEAD_DIM):
        cols = slice(head * HEAD_DIM, (head + 1) * HEAD_DIM)
        bias_head = bias_all[head]
        key_block = jnp.concatenate([first_key[:, cols], prev_key[:, cols]], 0)
        value_block = jnp.concatenate([first_value[:, cols], prev_value[:, cols]], 0)
        scores = jnp.dot(queries[:, cols], key_block.T, preferred_element_type=jnp.float32) * scale
        scores = (scores.reshape(cells, 2, cells) + bias_head[:, None, :]).reshape(cells, 2 * cells)
        peak = jnp.max(scores, axis=1, keepdims=True)
        weights = jnp.exp(scores - peak)
        probs = (weights / jnp.sum(weights, axis=1, keepdims=True)).astype(jnp.bfloat16)
        per_head.append(jnp.dot(probs, value_block, preferred_element_type=jnp.float32).astype(jnp.bfloat16))
    result = own.astype(jnp.float32)
    for head, attended in enumerate(per_head):
        rows = out_weight[head * HEAD_DIM : (head + 1) * HEAD_DIM]
        result = result + jnp.dot(attended, rows, preferred_element_type=jnp.float32)
    return result.astype(jnp.bfloat16).reshape(frames, cells, width)


def solution(mesh):
    return jax.shard_map(
        body,
        mesh=mesh,
        in_specs=(P(AXES, None, None), P(), P(), P(), P(), P(), P(), P(), P(), P()),
        out_specs=P(AXES, None, None),
        check_vma=False,
    )
```

```python
import numpy as np
import jax
import jax.numpy as jnp
from jax import lax
from jax.sharding import PartitionSpec as P

SIDE = 32
HEAD_DIM = 64
GROUPS = 32

EPS = 1e-05
AXES = ("seq", "sub")


def place_of():
    return lax.axis_index("seq") * lax.axis_size("sub") + lax.axis_index("sub")


def shifted(array, devices, by):
    pairs = [(i, i + by) for i in range(devices) if 0 <= i + by < devices]
    return lax.ppermute(array, AXES, pairs)


def butterfly_sum(x, devices, tied, tie_at):
    step = 1
    while step < devices:
        if step == tie_at:
            x, tied = lax.optimization_barrier((x, tied))
        x = x + lax.ppermute(x, AXES, [(i, i ^ step) for i in range(devices)])
        step *= 2
    return x, tied


def broadcast_pair(first, second, place, devices, work, step=2):
    done = []
    rounds = 0
    while step < devices:
        got_a = lax.ppermute(first, AXES, [(i, i + step) for i in range(0, step, 2)])
        got_b = lax.ppermute(second, AXES, [(i, i + step) for i in range(1, step, 2)])
        fresh = (place >= step) & (place < 2 * step)
        first = jnp.where(fresh & (place % 2 == 0), got_a, first)
        second = jnp.where(fresh & (place % 2 == 1), got_b, second)
        if rounds < len(work) and work[rounds] is not None:
            first, second, operand = lax.optimization_barrier((first, second, work[rounds][0]))
            done.append(work[rounds][1](operand))
        rounds += 1
        step *= 2
    for item in work[rounds:]:
        done.append(item[1](item[0]))
    swap_a = lax.ppermute(first, AXES, [(i, i ^ 1) for i in range(devices)])
    swap_b = lax.ppermute(second, AXES, [(i, i ^ 1) for i in range(devices)])
    even = place % 2 == 0
    return jnp.where(even, first, swap_a), jnp.where(even, swap_b, second), done


def bias_table(pos_table):
    heads, span, _ = pos_table.shape
    flipped = pos_table[:, ::-1, ::-1]
    coord = np.arange(SIDE)
    pick = np.arange(span)[:, None, None] == (SIDE - 1 - coord[:, None] + coord[None, :])[None]
    pick = jnp.asarray(pick.reshape(span, SIDE * SIDE), jnp.float32)
    table = jnp.einsum("hkj,jc->hkc", flipped, pick, precision=lax.Precision.HIGHEST)
    wide = jnp.transpose(table.reshape(heads, span, SIDE, SIDE), (0, 2, 1, 3))
    wide = wide.reshape(heads, SIDE, span * SIDE)
    return wide


def head_bias(wide_head):
    lanes = 128
    per = lanes // SIDE
    width = (SIDE - 1) // per * lanes + SIDE * SIDE
    shifted = [wide_head[:, SIDE * s : SIDE * s + width] for s in range(per)]
    rows = []
    for py in range(SIDE):
        start = (SIDE - 1 - py) * SIDE
        piece = shifted[start % lanes // SIDE]
        base = start // lanes * lanes
        rows.append(piece[:, base : base + SIDE * SIDE])
    return jnp.concatenate(rows, 0)


def project(rows, weight):
    return jnp.dot(rows, weight, preferred_element_type=jnp.float32).astype(jnp.bfloat16)


def body(
    latents,
    norm_gain,
    norm_bias,
    conv_weight,
    conv_bias,
    query_weight,
    key_weight,
    value_weight,
    out_weight,
    pos_table,
):
    frames, cells, width = latents.shape
    size = width // GROUPS
    devices = lax.axis_size("seq") * lax.axis_size("sub")
    place = place_of()
    own = latents[0]

    grouped = own.reshape(cells, GROUPS, size).astype(jnp.float32)
    partial = jnp.concatenate([jnp.sum(grouped, axis=(0, 2)), jnp.sum(grouped * grouped, axis=(0, 2))])
    got_a = lax.ppermute(own, AXES, [(0, 2)])
    got_b = lax.ppermute(own, AXES, [(1, 3)])
    start_a = jnp.where(place == 2, got_a, own)
    start_b = jnp.where(place == 3, got_b, own)
    stats, (start_a, start_b) = butterfly_sum(partial, devices, (start_a, start_b), 4)
    count = frames * devices * cells * size
    stats, pos_table, sent = lax.optimization_barrier((stats, pos_table, own))
    before = shifted(sent, devices, 1)
    before2 = shifted(sent, devices, 2)
    after = shifted(sent, devices, -1)
    wide = bias_table(pos_table)
    work = [(wide[h], head_bias) for h in range(wide.shape[0])]
    frame0, frame1, bias_all = broadcast_pair(start_a, start_b, place, devices, work, 4)
    mean = stats[:GROUPS] / count
    meansq = stats[GROUPS:] / count
    inv = lax.rsqrt(meansq - mean * mean + EPS)
    mean_c = jnp.repeat(mean, size)
    inv_c = jnp.repeat(inv, size)

    def norm(x):
        return ((x.astype(jnp.float32) - mean_c) * inv_c * norm_gain + norm_bias).astype(jnp.bfloat16)

    zero = jnp.zeros((cells, width), jnp.bfloat16)
    n_self = norm(own)
    n_before = jnp.where(place >= 1, norm(before), zero)
    n_before2 = jnp.where(place >= 2, norm(before2), zero)
    n_after = jnp.where(place + 1 < devices, norm(after), zero)
    n_0 = norm(frame0)
    n_1 = norm(frame1)

    taps = [
        jnp.concatenate([n_before2, n_before], 0),
        jnp.concatenate([n_before, n_self], 0),
        jnp.concatenate([n_self, n_after], 0),
    ]
    acc = jnp.zeros((2 * cells, width), jnp.float32)
    for tap in range(3):
        acc = acc + jnp.dot(taps[tap], conv_weight[tap], preferred_element_type=jnp.float32)
    mixed = (taps[1].astype(jnp.float32) + acc + conv_bias).astype(jnp.bfloat16)
    mixed_prev = mixed[:cells]
    mixed_self = mixed[cells:]
    acc0 = jnp.dot(n_0, conv_weight[1], preferred_element_type=jnp.float32)
    acc0 = acc0 + jnp.dot(n_1, conv_weight[2], preferred_element_type=jnp.float32)
    mixed_first = (n_0.astype(jnp.float32) + acc0 + conv_bias).astype(jnp.bfloat16)

    queries = project(mixed_self, query_weight)
    first_key = project(mixed_first, key_weight)
    first_value = project(mixed_first, value_weight)
    leading = place <= 1
    prev_key = jnp.where(leading, first_key, project(mixed_prev, key_weight))
    prev_value = jnp.where(leading, first_value, project(mixed_prev, value_weight))

    scale = HEAD_DIM ** (-0.5)
    per_head = []
    for head in range(width // HEAD_DIM):
        cols = slice(head * HEAD_DIM, (head + 1) * HEAD_DIM)
        bias_head = bias_all[head]
        key_block = jnp.concatenate([first_key[:, cols], prev_key[:, cols]], 0)
        value_block = jnp.concatenate([first_value[:, cols], prev_value[:, cols]], 0)
        scores = jnp.dot(queries[:, cols], key_block.T, preferred_element_type=jnp.float32) * scale
        scores = (scores.reshape(cells, 2, cells) + bias_head[:, None, :]).reshape(cells, 2 * cells)
        peak = jnp.max(scores, axis=1, keepdims=True)
        weights = jnp.exp(scores - peak)
        probs = (weights / jnp.sum(weights, axis=1, keepdims=True)).astype(jnp.bfloat16)
        per_head.append(jnp.dot(probs, value_block, preferred_element_type=jnp.float32).astype(jnp.bfloat16))
    attended = jnp.concatenate(per_head, 1)
    result = own.astype(jnp.float32) + jnp.dot(attended, out_weight, preferred_element_type=jnp.float32)
    return result.astype(jnp.bfloat16).reshape(frames, cells, width)


def solution(mesh):
    return jax.shard_map(
        body,
        mesh=mesh,
        in_specs=(P(AXES, None, None), P(), P(), P(), P(), P(), P(), P(), P(), P()),
        out_specs=P(AXES, None, None),
        check_vma=False,
    )
```
